128 devices in a mesh: sta: 32 (over z, y, x_lo), tm: 4 (over x_hi, core).
Axes of the slice: x: 4 (x_hi: 2, x_lo: 2; x = x_hi * 2 + x_lo), y: 4, z: 4, core: 2. Of those that a mesh axis runs over, the one named last changes fastest.
Arguments:
- signal: bfloat16 [1024, 12288], P('sta', 'tm'), may hold values from -6 to 6
- fir: float32 [4, 32], replicated, may hold values from -1 to 1
- taps: int32 [4], replicated, may hold values from 16 to 32, as said below
- sources: int32 [2, 16], replicated, may hold values from 0 to 1023, as said below
Outputs:
- correlations: bfloat16 [2, 4, 16, 1024, 512], P(None, None, None, 'sta', 'tm')
The draws below stay inside these ranges and needn't reach their ends.
Inputs may be any that keep to these rules, and one draw needn't show every extreme that they name: Each band has between 16 and 32 taps, and some band has exactly 32. `sources`: the source channels of one round are distinct.
All inputs are finite; a program needn't handle non-finite values.
Results may differ from the reference program's by a relative error of at most 0.0058.
Values may be sent and summed in bfloat16 or wider, within the bound.
No kernel may reach another device: no remote copies, remote signals or barrier semaphores. Data moves between devices by JAX's collectives and lax.ppermute only.
A program may use at most 128 MiB of HBM per device.

```python
import jax
import jax.numpy as jnp
from jax import lax

SOURCES = 16
ROUNDS = 2
BANDS = 4
TAPS_MAX = 32
MAXLAG = 256
LAGS = 512
CHANNELS = 1024
SAMPLES = 12288


def draw_taps(key, part):
    lower = jax.random.randint(key, (BANDS,), TAPS_MAX // 2, TAPS_MAX + 1)
    chosen = jax.random.randint(jax.random.fold_in(key, 7), (), 0, BANDS)
    return jnp.where(jnp.arange(BANDS) == chosen, TAPS_MAX, lower).astype(jnp.int32)


def draw_sources(key, part):
    round_keys = jax.random.split(key, ROUNDS)
    picked = jax.vmap(lambda single: jax.random.permutation(single, CHANNELS)[:SOURCES])(round_keys)
    return picked.astype(jnp.int32)


def block_scale(own_key, extent, cuts, smallest, largest):
    factor_of = 1.0
    for dim, shards_of in cuts:
        heights = jax.random.uniform(jax.random.fold_in(jax.random.fold_in(own_key, 6), dim), (shards_of,), jnp.float32, smallest / len(cuts), largest / len(cuts))
        factor_of = factor_of * jnp.repeat(jnp.exp(heights), extent[dim] // shards_of).reshape((-1,) + (1,) * (len(extent) - 1 - dim))
    return factor_of


def scatter_about(stream_key, shape, spread, most, shards=(), kind=jnp.bfloat16):
    result = jax.random.normal(stream_key, shape, jnp.float32) * spread
    if len(shards) > 0:
        result = block_scale(stream_key, shape, shards, -0.22, 0.18) * result
    return jnp.clip(result, min=-most, max=most).astype(kind)


def setup_inputs(seed: int = 0) -> dict:
    key_list = jax.random.split(jax.random.key(seed), 5)
    signal = scatter_about(key_list[0], (CHANNELS, SAMPLES), 1.0, 6.0, ((0, 32), (1, 4)))
    fir = scatter_about(key_list[1], (BANDS, TAPS_MAX), TAPS_MAX ** -0.5, 1.0, (), jnp.float32)
    taps = draw_taps(jax.random.fold_in(key_list[4], 71), 0)
    sources = draw_sources(jax.random.fold_in(key_list[4], 71), 0)
    return dict(signal=signal, fir=fir, taps=taps, sources=sources)


def skew(values, count_rows):
    leading = values.shape[:-1]
    length = values.shape[-1]
    row_width = length + count_rows
    padded = jnp.concatenate([values, jnp.zeros(leading + (count_rows,), values.dtype)], axis=-1)
    repeated = jnp.tile(padded, (1,) * len(leading) + (count_rows,))
    return repeated[..., : count_rows * (row_width - 1)].reshape(leading + (count_rows, row_width - 1))


def reference(signal, fir, taps, sources):
    active = jnp.arange(TAPS_MAX, dtype=jnp.int32)[None, :] < taps[:, None]
    coefficients = jnp.where(active, fir, 0.0).astype(jnp.bfloat16).astype(jnp.float32)
    traces = signal.astype(jnp.float32)
    padded = jnp.pad(traces, ((0, 0), (TAPS_MAX - 1, 0)))

    def one_band(weights):
        total = jnp.zeros(traces.shape, jnp.float32)
        for shift in range(TAPS_MAX):
            begin = TAPS_MAX - 1 - shift
            total = total + weights[shift] * padded[:, begin:begin + SAMPLES]
        return total.astype(jnp.bfloat16)

    filtered = lax.map(one_band, coefficients)
    norm_scale = SAMPLES ** -0.5
    rounds_out = []
    for rnd in range(ROUNDS):
        bands_out = []
        for band in range(BANDS):
            rows_band = filtered[band]
            picked = jnp.take(rows_band, sources[rnd], axis=0).astype(jnp.float32)
            hankel = skew(picked, LAGS)
            window = jnp.pad(rows_band, ((0, 0), (MAXLAG, MAXLAG)))[:, : SAMPLES + 2 * MAXLAG - 1].astype(jnp.float32)
            flat = hankel.reshape(SOURCES * LAGS, SAMPLES + 2 * MAXLAG - 1)
            product = jnp.dot(window, flat.T, preferred_element_type=jnp.float32) * norm_scale
            product = product.astype(jnp.bfloat16).reshape(CHANNELS, SOURCES, LAGS)
            bands_out.append(jnp.transpose(product, (1, 0, 2)))
        rounds_out.append(jnp.stack(bands_out, axis=0))
    return jnp.stack(rounds_out, axis=0)
```

```python
import functools

import jax
import jax.numpy as jnp
from jax import lax
from jax.experimental import pallas as pl
from jax.experimental.pallas import tpu as pltpu
from jax.sharding import PartitionSpec as P

ROUNDS = 2
MAXLAG = 256
SHIFTS = 16
CHUNK = 512


def skew(values, count_rows):
    leading = values.shape[:-1]
    length = values.shape[-1]
    row_width = length + count_rows
    padded = jnp.concatenate([values, jnp.zeros(leading + (count_rows,), values.dtype)], axis=-1)
    repeated = jnp.tile(padded, (1,) * len(leading) + (count_rows,))
    return repeated[..., : count_rows * (row_width - 1)].reshape(
        leading + (count_rows, row_width - 1)
    )


def band_matrix(fir, taps, count_rows):
    tap_limit = fir.shape[1]
    active = jnp.arange(tap_limit, dtype=jnp.int32)[None, :] < taps[:, None]
    coefficients = jnp.where(active, fir, 0.0).astype(jnp.bfloat16)
    return skew(coefficients[:, ::-1], count_rows)


def filter_blocks(extended, fir, taps, length, block):
    tap_limit = fir.shape[1]
    channels = extended.shape[0]
    count = length // block
    main = extended[:, tap_limit - 1 :].reshape(channels, count, block)
    prefix = extended[:, :length].reshape(channels, count, block)[:, :, : tap_limit - 1]
    pieces = jnp.concatenate([prefix, main], axis=2)
    result = jnp.einsum(
        "cnu,btu->bcnt", pieces, band_matrix(fir, taps, block), preferred_element_type=jnp.float32
    )
    return result.reshape(result.shape[0], channels, length)


def corr_kernel(fw_ref, pp_ref, out_ref, acc_ref, *, chunks, groups, rows_f, rows_p):
    acc_ref[...] = jnp.zeros_like(acc_ref)
    top = (groups - 1) * SHIFTS

    def step(k, carry):
        base = pl.multiple_of(k * CHUNK, CHUNK)
        fa = fw_ref[0, :, pl.ds(base, CHUNK + 128)]
        pa = pp_ref[0, :, pl.ds(base, CHUNK + 128)]
        lhs = jnp.concatenate([fa[:, q : q + CHUNK] for q in range(SHIFTS)], axis=0)
        rhs = jnp.concatenate(
            [pa[:, top - g * SHIFTS : top - g * SHIFTS + CHUNK] for g in range(groups)], axis=0
        )
        acc_ref[...] += lax.dot_general(
            lhs.astype(jnp.bfloat16),
            rhs.astype(jnp.bfloat16),
            (((1,), (1,)), ((), ())),
            preferred_element_type=jnp.float32,
        )
        return carry

    lax.fori_loop(0, chunks, step, 0)
    out_ref[0] = acc_ref[...]


def correlate(f_win, p_pad, lags, chunks):
    bands, rows_f, width = f_win.shape
    rows_p = p_pad.shape[1]
    groups = lags // SHIFTS
    kernel = functools.partial(
        corr_kernel, chunks=chunks, groups=groups, rows_f=rows_f, rows_p=rows_p
    )
    m = SHIFTS * rows_f
    n = groups * rows_p
    return pl.pallas_call(
        kernel,
        grid=(bands,),
        in_specs=[
            pl.BlockSpec((1, rows_f, width), lambda b: (b, 0, 0)),
            pl.BlockSpec((1, rows_p, width), lambda b: (b, 0, 0)),
        ],
        out_specs=pl.BlockSpec((1, m, n), lambda b: (b, 0, 0)),
        out_shape=jax.ShapeDtypeStruct((bands, m, n), jnp.float32),
        scratch_shapes=[pltpu.VMEM((m, n), jnp.float32)],
        compiler_params=pltpu.CompilerParams(vmem_limit_bytes=48 * 1024 * 1024),
    )(f_win, p_pad)


def per_device(signal, fir, taps, sources):
    channels = signal.shape[0]
    tap_limit = fir.shape[1]
    shards = lax.axis_size("tm")
    samples_all = signal.shape[1] * shards
    lag_count = 2 * MAXLAG
    share = lag_count // shards
    norm_scale = samples_all ** (-0.5)
    groups = share // SHIFTS
    count_src = sources.shape[1]

    flat_src = sources.reshape(-1)
    local_ids = flat_src - lax.axis_index("sta") * channels
    onehot = (local_ids[:, None] == jnp.arange(channels, dtype=jnp.int32)[None, :]).astype(
        jnp.bfloat16
    )
    picks = jnp.dot(onehot, signal, preferred_element_type=jnp.float32).astype(jnp.bfloat16)
    picks = lax.psum(picks, "sta")
    rows = jnp.concatenate([signal, picks], axis=0)
    rows = lax.all_gather(rows, "tm", axis=1, tiled=True)
    count_rows = rows.shape[0]
    extended = jnp.concatenate(
        [jnp.zeros((count_rows, tap_limit - 1), rows.dtype), rows], axis=1
    )
    filtered = filter_blocks(extended, fir, taps, samples_all, 256).astype(jnp.bfloat16)
    f_loc = filtered[:, :channels, :]
    p_src = filtered[:, channels:, :]

    span = samples_all + (groups - 1) * SHIFTS
    chunks = -(-span // CHUNK)
    width = chunks * CHUNK + 128
    f_big = jnp.pad(f_loc, ((0, 0), (0, 0), (MAXLAG, width - samples_all + lag_count)))
    start = lax.axis_index("tm") * share
    f_win = lax.dynamic_slice_in_dim(f_big, start, width, 2).astype(jnp.float32)
    top = (groups - 1) * SHIFTS
    p_pad = jnp.pad(p_src, ((0, 0), (0, 0), (top, width - samples_all - top))).astype(jnp.float32)

    out = correlate(f_win, p_pad, share, chunks)
    bands = out.shape[0]
    out = (out * norm_scale).astype(jnp.bfloat16)
    out = out.reshape(bands, SHIFTS, channels, groups, ROUNDS, count_src)
    out = jnp.transpose(out, (4, 0, 5, 2, 3, 1))
    return out.reshape(ROUNDS, bands, count_src, channels, share)


def solution(mesh):
    in_specs = (P("sta", "tm"), P(), P(), P())
    out_specs = P(None, None, None, "sta", "tm")
    return jax.shard_map(
        per_device, mesh=mesh, in_specs=in_specs, out_specs=out_specs, check_vma=False
    )
```

```python
import functools

import jax
import jax.numpy as jnp
from jax import lax
from jax.experimental import pallas as pl
from jax.experimental.pallas import tpu as pltpu
from jax.sharding import PartitionSpec as P

ROUNDS = 2
MAXLAG = 256
SHIFTS = 16
CHUNK = 512


def skew(values, count_rows):
    leading = values.shape[:-1]
    length = values.shape[-1]
    row_width = length + count_rows
    padded = jnp.concatenate([values, jnp.zeros(leading + (count_rows,), values.dtype)], axis=-1)
    repeated = jnp.tile(padded, (1,) * len(leading) + (count_rows,))
    return repeated[..., : count_rows * (row_width - 1)].reshape(
        leading + (count_rows, row_width - 1)
    )


def band_matrix(fir, taps, count_rows):
    tap_limit = fir.shape[1]
    active = jnp.arange(tap_limit, dtype=jnp.int32)[None, :] < taps[:, None]
    coefficients = jnp.where(active, fir, 0.0).astype(jnp.bfloat16)
    return skew(coefficients[:, ::-1], count_rows)


def filter_blocks(extended, fir, taps, length, block):
    tap_limit = fir.shape[1]
    channels = extended.shape[0]
    count = length // block
    main = extended[:, tap_limit - 1 :].reshape(channels, count, block)
    prefix = extended[:, :length].reshape(channels, count, block)[:, :, : tap_limit - 1]
    pieces = jnp.concatenate([prefix, main], axis=2)
    result = jnp.einsum(
        "cnu,btu->bcnt", pieces, band_matrix(fir, taps, block), preferred_element_type=jnp.float32
    )
    return result.reshape(result.shape[0], channels, length)


def corr_kernel(fw_ref, pp_ref, out_ref, acc_ref, *, chunks, groups, rows_f, rows_p):
    acc_ref[...] = jnp.zeros_like(acc_ref)
    top = (groups - 1) * SHIFTS

    def step(k, carry):
        base = pl.multiple_of(k * CHUNK, CHUNK)
        fa = fw_ref[0, :, pl.ds(base, CHUNK + 128)]
        pa = pp_ref[0, :, pl.ds(base, CHUNK + 128)]
        lhs = jnp.concatenate([fa[:, q : q + CHUNK] for q in range(SHIFTS)], axis=0)
        rhs = jnp.concatenate(
            [pa[:, top - g * SHIFTS : top - g * SHIFTS + CHUNK] for g in range(groups)], axis=0
        )
        acc_ref[...] += lax.dot_general(
            lhs.astype(jnp.bfloat16),
            rhs.astype(jnp.bfloat16),
            (((1,), (1,)), ((), ())),
            preferred_element_type=jnp.float32,
        )
        return carry

    lax.fori_loop(0, chunks, step, 0)
    out_ref[0] = acc_ref[...]


def correlate(f_win, p_pad, lags, chunks):
    bands, rows_f, width = f_win.shape
    rows_p = p_pad.shape[1]
    groups = lags // SHIFTS
    kernel = functools.partial(
        corr_kernel, chunks=chunks, groups=groups, rows_f=rows_f, rows_p=rows_p
    )
    m = SHIFTS * rows_f
    n = groups * rows_p
    return pl.pallas_call(
        kernel,
        grid=(bands,),
        in_specs=[
            pl.BlockSpec((1, rows_f, width), lambda b: (b, 0, 0)),
            pl.BlockSpec((1, rows_p, width), lambda b: (b, 0, 0)),
        ],
        out_specs=pl.BlockSpec((1, m, n), lambda b: (b, 0, 0)),
        out_shape=jax.ShapeDtypeStruct((bands, m, n), jnp.float32),
        scratch_shapes=[pltpu.VMEM((m, n), jnp.float32)],
        compiler_params=pltpu.CompilerParams(vmem_limit_bytes=48 * 1024 * 1024),
    )(f_win, p_pad)


def summed_over(value, axis):
    count = lax.axis_size(axis)
    step = 1
    while step < count:
        value = value + lax.ppermute(value, axis, [(i, i ^ step) for i in range(count)])
        step *= 2
    return value


def per_device(signal, fir, taps, sources):
    channels = signal.shape[0]
    tap_limit = fir.shape[1]
    shards = lax.axis_size("tm")
    samples_all = signal.shape[1] * shards
    lag_count = 2 * MAXLAG
    share = lag_count // shards
    norm_scale = samples_all ** (-0.5)
    groups = share // SHIFTS
    count_src = sources.shape[1]

    flat_src = sources.reshape(-1)
    local_ids = flat_src - lax.axis_index("sta") * channels
    onehot = (local_ids[:, None] == jnp.arange(channels, dtype=jnp.int32)[None, :]).astype(
        jnp.bfloat16
    )
    picks = jnp.dot(onehot, signal, preferred_element_type=jnp.float32).astype(jnp.bfloat16)
    picks = summed_over(picks, "sta")

    def filtered_of(rows):
        rows = lax.all_gather(rows, "tm", axis=1, tiled=True)
        extended = jnp.concatenate(
            [jnp.zeros((rows.shape[0], tap_limit - 1), rows.dtype), rows], axis=1
        )
        return filter_blocks(extended, fir, taps, samples_all, 256).astype(jnp.bfloat16)

    f_loc = filtered_of(signal)
    p_src = filtered_of(picks)

    span = samples_all + (groups - 1) * SHIFTS
    chunks = -(-span // CHUNK)
    width = chunks * CHUNK + 128
    f_big = jnp.pad(f_loc, ((0, 0), (0, 0), (MAXLAG, width - samples_all + lag_count)))
    start = lax.axis_index("tm") * share
    f_win = lax.dynamic_slice_in_dim(f_big, start, width, 2).astype(jnp.float32)
    top = (groups - 1) * SHIFTS
    p_pad = jnp.pad(p_src, ((0, 0), (0, 0), (top, width - samples_all - top))).astype(jnp.float32)

    out = correlate(f_win, p_pad, share, chunks)
    bands = out.shape[0]
    out = (out * norm_scale).astype(jnp.bfloat16)
    out = out.reshape(bands, SHIFTS, channels, groups, ROUNDS, count_src)
    out = jnp.transpose(out, (4, 0, 5, 2, 3, 1))
    return out.reshape(ROUNDS, bands, count_src, channels, share)


def solution(mesh):
    in_specs = (P("sta", "tm"), P(), P(), P())
    out_specs = P(None, None, None, "sta", "tm")
    return jax.shard_map(
        per_device, mesh=mesh, in_specs=in_specs, out_specs=out_specs, check_vma=False
    )
```

```python
import functools

import jax
import jax.numpy as jnp
from jax import lax
from jax.experimental import pallas as pl
from jax.experimental.pallas import tpu as pltpu
from jax.sharding import PartitionSpec as P

ROUNDS = 2
MAXLAG = 256
SHIFTS = 16
CHUNK = 512


def skew(values, count_rows):
    leading = values.shape[:-1]
    length = values.shape[-1]
    row_width = length + count_rows
    padded = jnp.concatenate([values, jnp.zeros(leading + (count_rows,), values.dtype)], axis=-1)
    repeated = jnp.tile(padded, (1,) * len(leading) + (count_rows,))
    return repeated[..., : count_rows * (row_width - 1)].reshape(
        leading + (count_rows, row_width - 1)
    )


def band_matrix(fir, taps, count_rows):
    tap_limit = fir.shape[1]
    active = jnp.arange(tap_limit, dtype=jnp.int32)[None, :] < taps[:, None]
    coefficients = jnp.where(active, fir, 0.0).astype(jnp.bfloat16)
    return skew(coefficients[:, ::-1], count_rows)


def filter_blocks(extended, fir, taps, length, block):
    tap_limit = fir.shape[1]
    channels = extended.shape[0]
    count = length // block
    main = extended[:, tap_limit - 1 :].reshape(channels, count, block)
    prefix = extended[:, :length].reshape(channels, count, block)[:, :, : tap_limit - 1]
    pieces = jnp.concatenate([prefix, main], axis=2)
    result = jnp.einsum(
        "cnu,btu->bcnt", pieces, band_matrix(fir, taps, block), preferred_element_type=jnp.float32
    )
    return result.reshape(result.shape[0], channels, length)


def corr_kernel(fw_ref, pp_ref, out_ref, acc_ref, *, chunks, groups, rows_f, rows_p):
    acc_ref[...] = jnp.zeros_like(acc_ref)
    top = (groups - 1) * SHIFTS

    def step(k, carry):
        base = pl.multiple_of(k * CHUNK, CHUNK)
        fa = fw_ref[0, :, pl.ds(base, CHUNK + 128)]
        pa = pp_ref[0, :, pl.ds(base, CHUNK + 128)]
        lhs = jnp.concatenate([fa[:, q : q + CHUNK] for q in range(SHIFTS)], axis=0)
        rhs = jnp.concatenate(
            [pa[:, top - g * SHIFTS : top - g * SHIFTS + CHUNK] for g in range(groups)], axis=0
        )
        acc_ref[...] += lax.dot_general(
            lhs.astype(jnp.bfloat16),
            rhs.astype(jnp.bfloat16),
            (((1,), (1,)), ((), ())),
            preferred_element_type=jnp.float32,
        )
        return carry

    lax.fori_loop(0, chunks, step, 0)
    out_ref[0] = acc_ref[...]


def correlate(f_win, p_pad, lags, chunks):
    bands, rows_f, width = f_win.shape
    rows_p = p_pad.shape[1]
    groups = lags // SHIFTS
    kernel = functools.partial(
        corr_kernel, chunks=chunks, groups=groups, rows_f=rows_f, rows_p=rows_p
    )
    m = SHIFTS * rows_f
    n = groups * rows_p
    return pl.pallas_call(
        kernel,
        grid=(bands,),
        in_specs=[
            pl.BlockSpec((1, rows_f, width), lambda b: (b, 0, 0)),
            pl.BlockSpec((1, rows_p, width), lambda b: (b, 0, 0)),
        ],
        out_specs=pl.BlockSpec((1, m, n), lambda b: (b, 0, 0)),
        out_shape=jax.ShapeDtypeStruct((bands, m, n), jnp.float32),
        scratch_shapes=[pltpu.VMEM((m, n), jnp.float32)],
        compiler_params=pltpu.CompilerParams(vmem_limit_bytes=48 * 1024 * 1024),
    )(f_win, p_pad)


def summed_over(value, axis):
    count = lax.axis_size(axis)
    step = 1
    while step < count:
        value = value + lax.ppermute(value, axis, [(i, i ^ step) for i in range(count)])
        step *= 2
    return value


def per_device(signal, fir, taps, sources):
    channels = signal.shape[0]
    tap_limit = fir.shape[1]
    shards = lax.axis_size("tm")
    samples_all = signal.shape[1] * shards
    lag_count = 2 * MAXLAG
    share = lag_count // shards
    norm_scale = samples_all ** (-0.5)
    groups = share // SHIFTS
    count_src = sources.shape[1]

    flat_src = sources.reshape(-1)
    local_ids = flat_src - lax.axis_index("sta") * channels
    onehot = (local_ids[:, None] == jnp.arange(channels, dtype=jnp.int32)[None, :]).astype(
        jnp.bfloat16
    )
    picks = jnp.dot(onehot, signal, preferred_element_type=jnp.float32).astype(jnp.bfloat16)
    picks = summed_over(picks, "sta")

    def filtered_of(rows):
        rows = lax.all_gather(rows, "tm", axis=1, tiled=True)
        extended = jnp.concatenate(
            [jnp.zeros((rows.shape[0], tap_limit - 1), rows.dtype), rows], axis=1
        )
        return filter_blocks(extended, fir, taps, samples_all, 256).astype(jnp.bfloat16)

    f_loc = filtered_of(signal)
    p_src = filtered_of(picks)

    span = samples_all + (groups - 1) * SHIFTS
    chunks = -(-span // CHUNK)
    width = chunks * CHUNK + 128
    f_big = jnp.pad(f_loc, ((0, 0), (0, 0), (MAXLAG, width - samples_all + lag_count)))
    start = lax.axis_index("tm") * share
    f_win = lax.dynamic_slice_in_dim(f_big, start, width, 2)
    top = (groups - 1) * SHIFTS
    p_pad = jnp.pad(p_src, ((0, 0), (0, 0), (top, width - samples_all - top)))

    out = correlate(f_win, p_pad, share, chunks)
    bands = out.shape[0]
    out = (out * norm_scale).astype(jnp.bfloat16)
    out = out.reshape(bands, SHIFTS, channels, groups, ROUNDS, count_src)
    out = jnp.transpose(out, (4, 0, 5, 2, 3, 1))
    return out.reshape(ROUNDS, bands, count_src, channels, share)


def solution(mesh):
    in_specs = (P("sta", "tm"), P(), P(), P())
    out_specs = P(None, None, None, "sta", "tm")
    return jax.shard_map(
        per_device, mesh=mesh, in_specs=in_specs, out_specs=out_specs, check_vma=False
    )
```

```python
import functools

import jax
import jax.numpy as jnp
from jax import lax
from jax.experimental import pallas as pl
from jax.experimental.pallas import tpu as pltpu
from jax.sharding import PartitionSpec as P

ROUNDS = 2
MAXLAG = 256
SHIFTS = 16
CHUNK = 2560


def skew(values, count_rows):
    leading = values.shape[:-1]
    length = values.shape[-1]
    row_width = length + count_rows
    padded = jnp.concatenate([values, jnp.zeros(leading + (count_rows,), values.dtype)], axis=-1)
    repeated = jnp.tile(padded, (1,) * len(leading) + (count_rows,))
    return repeated[..., : count_rows * (row_width - 1)].reshape(
        leading + (count_rows, row_width - 1)
    )


def band_matrix(fir, taps, count_rows):
    tap_limit = fir.shape[1]
    active = jnp.arange(tap_limit, dtype=jnp.int32)[None, :] < taps[:, None]
    coefficients = jnp.where(active, fir, 0.0).astype(jnp.bfloat16)
    return skew(coefficients[:, ::-1], count_rows)


def filter_blocks(extended, fir, taps, length, block):
    tap_limit = fir.shape[1]
    channels = extended.shape[0]
    count = length // block
    main = extended[:, tap_limit - 1 :].reshape(channels, count, block)
    prefix = extended[:, :length].reshape(channels, count, block)[:, :, : tap_limit - 1]
    pieces = jnp.concatenate([prefix, main], axis=2)
    result = jnp.einsum(
        "cnu,btu->bcnt", pieces, band_matrix(fir, taps, block), preferred_element_type=jnp.float32
    )
    return result.reshape(result.shape[0], channels, length)


def corr_kernel(fw_ref, pp_ref, out_ref, acc_ref, *, chunks, groups, rows_f, rows_p):
    acc_ref[...] = jnp.zeros_like(acc_ref)
    top = (groups - 1) * SHIFTS

    def step(k, carry):
        base = pl.multiple_of(k * CHUNK, CHUNK)
        fa = fw_ref[0, :, pl.ds(base, CHUNK + 128)]
        pa = pp_ref[0, :, pl.ds(base, CHUNK + 128)]
        lhs = jnp.concatenate([fa[:, q : q + CHUNK] for q in range(SHIFTS)], axis=0)
        rhs = jnp.concatenate(
            [pa[:, top - g * SHIFTS : top - g * SHIFTS + CHUNK] for g in range(groups)], axis=0
        )
        acc_ref[...] += lax.dot_general(
            lhs.astype(jnp.bfloat16),
            rhs.astype(jnp.bfloat16),
            (((1,), (1,)), ((), ())),
            preferred_element_type=jnp.float32,
        )
        return carry

    lax.fori_loop(0, chunks, step, 0)
    out_ref[0] = acc_ref[...]


def correlate(f_win, p_pad, lags, chunks):
    bands, rows_f, width = f_win.shape
    rows_p = p_pad.shape[1]
    groups = lags // SHIFTS
    kernel = functools.partial(
        corr_kernel, chunks=chunks, groups=groups, rows_f=rows_f, rows_p=rows_p
    )
    m = SHIFTS * rows_f
    n = groups * rows_p
    return pl.pallas_call(
        kernel,
        grid=(bands,),
        in_specs=[
            pl.BlockSpec((1, rows_f, width), lambda b: (b, 0, 0)),
            pl.BlockSpec((1, rows_p, width), lambda b: (b, 0, 0)),
        ],
        out_specs=pl.BlockSpec((1, m, n), lambda b: (b, 0, 0)),
        out_shape=jax.ShapeDtypeStruct((bands, m, n), jnp.float32),
        scratch_shapes=[pltpu.VMEM((m, n), jnp.float32)],
        compiler_params=pltpu.CompilerParams(vmem_limit_bytes=48 * 1024 * 1024),
    )(f_win, p_pad)


def summed_over(value, axis):
    count = lax.axis_size(axis)
    bits = max(1, (count - 1).bit_length())
    rounds = [[0]] + [list(range(b, min(b + 2, bits))) for b in range(1, bits, 2)]
    for group in rounds:
        masks = [
            m for m in range(1, count)
            if all((m >> b) & 1 == 0 for b in range(bits) if b not in group)
        ]
        parts = [lax.ppermute(value, axis, [(i, i ^ m) for i in range(count)]) for m in masks]
        value = sum(parts, value)
    return value


def per_device(signal, fir, taps, sources):
    channels = signal.shape[0]
    tap_limit = fir.shape[1]
    shards = lax.axis_size("tm")
    samples_all = signal.shape[1] * shards
    lag_count = 2 * MAXLAG
    share = lag_count // shards
    norm_scale = samples_all ** (-0.5)
    groups = share // SHIFTS
    count_src = sources.shape[1]

    flat_src = sources.reshape(-1)
    local_ids = flat_src - lax.axis_index("sta") * channels
    onehot = (local_ids[:, None] == jnp.arange(channels, dtype=jnp.int32)[None, :]).astype(
        jnp.bfloat16
    )
    picks = jnp.dot(onehot, signal, preferred_element_type=jnp.float32).astype(jnp.bfloat16)
    picks = summed_over(picks, "sta")

    def filtered_of(rows):
        rows = lax.all_gather(rows, "tm", axis=1, tiled=True)
        extended = jnp.concatenate(
            [jnp.zeros((rows.shape[0], tap_limit - 1), rows.dtype), rows], axis=1
        )
        return filter_blocks(extended, fir, taps, samples_all, 256).astype(jnp.bfloat16)

    f_loc = filtered_of(signal)
    p_src = filtered_of(picks)

    span = samples_all + (groups - 1) * SHIFTS
    chunks = -(-span // CHUNK)
    width = chunks * CHUNK + 128
    f_big = jnp.pad(f_loc, ((0, 0), (0, 0), (MAXLAG, width - samples_all + lag_count)))
    start = lax.axis_index("tm") * share
    f_win = lax.dynamic_slice_in_dim(f_big, start, width, 2)
    top = (groups - 1) * SHIFTS
    p_pad = jnp.pad(p_src, ((0, 0), (0, 0), (top, width - samples_all - top)))

    out = correlate(f_win, p_pad, share, chunks)
    bands = out.shape[0]
    out = (out * norm_scale).astype(jnp.bfloat16)
    out = out.reshape(bands, SHIFTS, channels, groups, ROUNDS, count_src)
    out = jnp.transpose(out, (4, 0, 5, 2, 3, 1))
    return out.reshape(ROUNDS, bands, count_src, channels, share)


def solution(mesh):
    in_specs = (P("sta", "tm"), P(), P(), P())
    out_specs = P(None, None, None, "sta", "tm")
    return jax.shard_map(
        per_device, mesh=mesh, in_specs=in_specs, out_specs=out_specs, check_vma=False
    )
```

```python
import functools

import jax
import jax.numpy as jnp
from jax import lax
from jax.experimental import pallas as pl
from jax.experimental.pallas import tpu as pltpu
from jax.sharding import PartitionSpec as P

ROUNDS = 2
MAXLAG = 256
SHIFTS = 16
CHUNK = 2560


def skew(values, count_rows):
    leading = values.shape[:-1]
    length = values.shape[-1]
    row_width = length + count_rows
    padded = jnp.concatenate([values, jnp.zeros(leading + (count_rows,), values.dtype)], axis=-1)
    repeated = jnp.tile(padded, (1,) * len(leading) + (count_rows,))
    return repeated[..., : count_rows * (row_width - 1)].reshape(
        leading + (count_rows, row_width - 1)
    )


def band_matrix(fir, taps, count_rows):
    tap_limit = fir.shape[1]
    active = jnp.arange(tap_limit, dtype=jnp.int32)[None, :] < taps[:, None]
    coefficients = jnp.where(active, fir, 0.0).astype(jnp.bfloat16)
    return skew(coefficients[:, ::-1], count_rows)


def filter_blocks(extended, fir, taps, length, block):
    tap_limit = fir.shape[1]
    channels = extended.shape[0]
    count = length // block
    main = extended[:, tap_limit - 1 :].reshape(channels, count, block)
    prefix = extended[:, :length].reshape(channels, count, block)[:, :, : tap_limit - 1]
    pieces = jnp.concatenate([prefix, main], axis=2)
    return jnp.einsum(
        "cnu,btu->bnct", pieces, band_matrix(fir, taps, block), preferred_element_type=jnp.float32
    )


def corr_kernel(off_ref, fw_ref, pp_ref, out_ref, acc_ref, *, chunks, groups, scale):
    acc_ref[...] = jnp.zeros_like(acc_ref)
    per = CHUNK // 128
    off = off_ref[0]

    def step(k, carry):
        first = k * per
        fa = jnp.concatenate([fw_ref[0, off + first + i] for i in range(per + 1)], axis=1)
        pa = jnp.concatenate([pp_ref[0, first + i] for i in range(per + 1)], axis=1)
        lhs = jnp.concatenate([fa[:, q : q + CHUNK] for q in range(SHIFTS)], axis=0)
        rhs = jnp.concatenate(
            [pa[:, 128 - g * SHIFTS : 128 - g * SHIFTS + CHUNK] for g in range(groups)], axis=0
        )
        acc_ref[...] += lax.dot_general(
            lhs, rhs, (((1,), (1,)), ((), ())), preferred_element_type=jnp.float32
        )
        return carry

    lax.fori_loop(0, chunks, step, 0)
    out_ref[0] = (acc_ref[...] * scale).astype(out_ref.dtype)


def correlate(offset, f_blocks, p_blocks, lags, chunks, scale):
    bands, nf, rows_f, _ = f_blocks.shape
    np_, rows_p = p_blocks.shape[1], p_blocks.shape[2]
    groups = lags // SHIFTS
    kernel = functools.partial(corr_kernel, chunks=chunks, groups=groups, scale=scale)
    m = SHIFTS * rows_f
    n = groups * rows_p
    grid_spec = pltpu.PrefetchScalarGridSpec(
        num_scalar_prefetch=1,
        grid=(bands,),
        in_specs=[
            pl.BlockSpec((1, nf, rows_f, 128), lambda b, o: (b, 0, 0, 0)),
            pl.BlockSpec((1, np_, rows_p, 128), lambda b, o: (b, 0, 0, 0)),
        ],
        out_specs=pl.BlockSpec((1, m, n), lambda b, o: (b, 0, 0)),
        scratch_shapes=[pltpu.VMEM((m, n), jnp.float32)],
    )
    return pl.pallas_call(
        kernel,
        grid_spec=grid_spec,
        out_shape=jax.ShapeDtypeStruct((bands, m, n), jnp.bfloat16),
        compiler_params=pltpu.CompilerParams(vmem_limit_bytes=48 * 1024 * 1024),
    )(offset, f_blocks, p_blocks)


def summed_over(value, axis):
    count = lax.axis_size(axis)
    bits = max(1, (count - 1).bit_length())
    rounds = [[0]] + [list(range(b, min(b + 2, bits))) for b in range(1, bits, 2)]
    for group in rounds:
        masks = [
            m for m in range(1, count)
            if all((m >> b) & 1 == 0 for b in range(bits) if b not in group)
        ]
        parts = [lax.ppermute(value, axis, [(i, i ^ m) for i in range(count)]) for m in masks]
        value = sum(parts, value)
    return value


def per_device(signal, fir, taps, sources):
    channels = signal.shape[0]
    tap_limit = fir.shape[1]
    shards = lax.axis_size("tm")
    samples_all = signal.shape[1] * shards
    lag_count = 2 * MAXLAG
    share = lag_count // shards
    norm_scale = samples_all ** (-0.5)
    groups = share // SHIFTS
    count_src = sources.shape[1]

    flat_src = sources.reshape(-1)
    local_ids = flat_src - lax.axis_index("sta") * channels
    onehot = (local_ids[:, None] == jnp.arange(channels, dtype=jnp.int32)[None, :]).astype(
        jnp.bfloat16
    )
    picks = jnp.dot(onehot, signal, preferred_element_type=jnp.float32).astype(jnp.bfloat16)
    picks = summed_over(picks, "sta")

    def filtered_of(rows):
        rows = lax.all_gather(rows, "tm", axis=1, tiled=True)
        extended = jnp.concatenate(
            [jnp.zeros((rows.shape[0], tap_limit - 1), rows.dtype), rows], axis=1
        )
        return filter_blocks(extended, fir, taps, samples_all, 128).astype(jnp.bfloat16)

    f_loc = filtered_of(signal)
    p_src = filtered_of(picks)

    span = samples_all + (groups - 1) * SHIFTS
    chunks = -(-span // CHUNK)
    blocks = chunks * CHUNK // 128 + 1
    data_blocks = samples_all // 128
    f_front = MAXLAG // 128
    f_blocks = jnp.pad(
        f_loc, ((0, 0), (f_front, blocks + lag_count // 128 - data_blocks - f_front), (0, 0), (0, 0))
    )
    p_blocks = jnp.pad(p_src, ((0, 0), (1, blocks - data_blocks - 1), (0, 0), (0, 0)))
    offset = (lax.axis_index("tm") * (share // 128)).astype(jnp.int32).reshape(1)

    out = correlate(offset, f_blocks, p_blocks, share, chunks, norm_scale)
    bands = out.shape[0]
    out = out.reshape(bands, SHIFTS, channels, groups, ROUNDS, count_src)
    out = jnp.transpose(out, (4, 0, 5, 2, 3, 1))
    return out.reshape(ROUNDS, bands, count_src, channels, share)


def solution(mesh):
    in_specs = (P("sta", "tm"), P(), P(), P())
    out_specs = P(None, None, None, "sta", "tm")
    return jax.shard_map(
        per_device, mesh=mesh, in_specs=in_specs, out_specs=out_specs, check_vma=False
    )
```

```python
import functools

import jax
import jax.numpy as jnp
from jax import lax
from jax.experimental import pallas as pl
from jax.experimental.pallas import tpu as pltpu
from jax.sharding import PartitionSpec as P

ROUNDS = 2
MAXLAG = 256
SHIFTS = 16
CHUNK = 2560


def skew(values, count_rows):
    leading = values.shape[:-1]
    length = values.shape[-1]
    row_width = length + count_rows
    padded = jnp.concatenate([values, jnp.zeros(leading + (count_rows,), values.dtype)], axis=-1)
    repeated = jnp.tile(padded, (1,) * len(leading) + (count_rows,))
    return repeated[..., : count_rows * (row_width - 1)].reshape(
        leading + (count_rows, row_width - 1)
    )


def band_matrix(fir, taps, count_rows):
    tap_limit = fir.shape[1]
    active = jnp.arange(tap_limit, dtype=jnp.int32)[None, :] < taps[:, None]
    coefficients = jnp.where(active, fir, 0.0).astype(jnp.bfloat16)
    return skew(coefficients[:, ::-1], count_rows)


def filter_blocks(extended, fir, taps, length, block):
    tap_limit = fir.shape[1]
    channels = extended.shape[0]
    count = length // block
    main = extended[:, tap_limit - 1 :].reshape(channels, count, block)
    prefix = extended[:, :length].reshape(channels, count, block)[:, :, : tap_limit - 1]
    pieces = jnp.concatenate([prefix, main], axis=2)
    return jnp.einsum(
        "cnu,btu->bnct", pieces, band_matrix(fir, taps, block), preferred_element_type=jnp.float32
    )


def corr_kernel(off_ref, fw_ref, pp_ref, out_ref, acc_ref, *, chunks, groups, scale):
    acc_ref[...] = jnp.zeros_like(acc_ref)
    per = CHUNK // 128
    off = off_ref[0]

    def step(k, carry):
        first = k * per
        fa = jnp.concatenate([fw_ref[0, off + first + i] for i in range(per + 1)], axis=1)
        pa = jnp.concatenate([pp_ref[0, first + i] for i in range(per + 1)], axis=1)
        lhs = jnp.concatenate([fa[:, q : q + CHUNK] for q in range(SHIFTS)], axis=0)
        rhs = jnp.concatenate(
            [pa[:, 128 - g * SHIFTS : 128 - g * SHIFTS + CHUNK] for g in range(groups)], axis=0
        )
        acc_ref[...] += lax.dot_general(
            lhs, rhs, (((1,), (1,)), ((), ())), preferred_element_type=jnp.float32
        )
        return carry

    lax.fori_loop(0, chunks, step, 0)
    out_ref[0] = (acc_ref[...] * scale).astype(out_ref.dtype)


def correlate(offset, f_blocks, p_blocks, lags, chunks, scale):
    bands, nf, rows_f, _ = f_blocks.shape
    np_, rows_p = p_blocks.shape[1], p_blocks.shape[2]
    groups = lags // SHIFTS
    kernel = functools.partial(corr_kernel, chunks=chunks, groups=groups, scale=scale)
    m = SHIFTS * rows_f
    n = groups * rows_p
    grid_spec = pltpu.PrefetchScalarGridSpec(
        num_scalar_prefetch=1,
        grid=(bands,),
        in_specs=[
            pl.BlockSpec((1, nf, rows_f, 128), lambda b, o: (b, 0, 0, 0)),
            pl.BlockSpec((1, np_, rows_p, 128), lambda b, o: (b, 0, 0, 0)),
        ],
        out_specs=pl.BlockSpec((1, m, n), lambda b, o: (b, 0, 0)),
        scratch_shapes=[pltpu.VMEM((m, n), jnp.float32)],
    )
    return pl.pallas_call(
        kernel,
        grid_spec=grid_spec,
        out_shape=jax.ShapeDtypeStruct((bands, m, n), jnp.bfloat16),
        compiler_params=pltpu.CompilerParams(vmem_limit_bytes=48 * 1024 * 1024),
    )(offset, f_blocks, p_blocks)


def summed_over(value, axis):
    count = lax.axis_size(axis)
    bits = max(1, (count - 1).bit_length())
    rounds = [[0]] + [list(range(b, min(b + 2, bits))) for b in range(1, bits, 2)]
    for group in rounds:
        masks = [
            m for m in range(1, count)
            if all((m >> b) & 1 == 0 for b in range(bits) if b not in group)
        ]
        parts = [lax.ppermute(value, axis, [(i, i ^ m) for i in range(count)]) for m in masks]
        value = sum(parts, value)
    return value


def per_device(signal, fir, taps, sources):
    channels = signal.shape[0]
    tap_limit = fir.shape[1]
    shards = lax.axis_size("tm")
    samples_all = signal.shape[1] * shards
    lag_count = 2 * MAXLAG
    share = lag_count // shards
    norm_scale = samples_all ** (-0.5)
    groups = share // SHIFTS
    count_src = sources.shape[1]

    flat_src = sources.reshape(-1)
    local_ids = flat_src - lax.axis_index("sta") * channels
    onehot = (local_ids[:, None] == jnp.arange(channels, dtype=jnp.int32)[None, :]).astype(
        jnp.bfloat16
    )
    picks = jnp.dot(onehot, signal, preferred_element_type=jnp.float32).astype(jnp.bfloat16)
    picks = summed_over(picks, "sta")

    def filtered_of(rows):
        rows = lax.all_gather(rows, "tm", axis=1, tiled=True)
        extended = jnp.concatenate(
            [jnp.zeros((rows.shape[0], tap_limit - 1), rows.dtype), rows], axis=1
        )
        return filter_blocks(extended, fir, taps, samples_all, 128).astype(jnp.bfloat16)

    both = filtered_of(jnp.concatenate([signal, picks], axis=0))
    f_loc = both[:, :, :channels]
    p_src = both[:, :, channels:]

    span = samples_all + (groups - 1) * SHIFTS
    chunks = -(-span // CHUNK)
    blocks = chunks * CHUNK // 128 + 1
    data_blocks = samples_all // 128
    f_front = MAXLAG // 128
    f_blocks = jnp.pad(
        f_loc, ((0, 0), (f_front, blocks + lag_count // 128 - data_blocks - f_front), (0, 0), (0, 0))
    )
    p_blocks = jnp.pad(p_src, ((0, 0), (1, blocks - data_blocks - 1), (0, 0), (0, 0)))
    offset = (lax.axis_index("tm") * (share // 128)).astype(jnp.int32).reshape(1)

    out = correlate(offset, f_blocks, p_blocks, share, chunks, norm_scale)
    bands = out.shape[0]
    out = out.reshape(bands, SHIFTS, channels, groups, ROUNDS, count_src)
    out = jnp.transpose(out, (4, 0, 5, 2, 3, 1))
    return out.reshape(ROUNDS, bands, count_src, channels, share)


def solution(mesh):
    in_specs = (P("sta", "tm"), P(), P(), P())
    out_specs = P(None, None, None, "sta", "tm")
    return jax.shard_map(
        per_device, mesh=mesh, in_specs=in_specs, out_specs=out_specs, check_vma=False
    )
```

```python
import functools

import jax
import jax.numpy as jnp
from jax import lax
from jax.experimental import pallas as pl
from jax.experimental.pallas import tpu as pltpu
from jax.sharding import PartitionSpec as P

ROUNDS = 2
MAXLAG = 256
SHIFTS = 16
CHUNK = 2560


def skew(values, count_rows):
    leading = values.shape[:-1]
    length = values.shape[-1]
    row_width = length + count_rows
    padded = jnp.concatenate([values, jnp.zeros(leading + (count_rows,), values.dtype)], axis=-1)
    repeated = jnp.tile(padded, (1,) * len(leading) + (count_rows,))
    return repeated[..., : count_rows * (row_width - 1)].reshape(
        leading + (count_rows, row_width - 1)
    )


def band_matrix(fir, taps, count_rows):
    tap_limit = fir.shape[1]
    active = jnp.arange(tap_limit, dtype=jnp.int32)[None, :] < taps[:, None]
    coefficients = jnp.where(active, fir, 0.0).astype(jnp.bfloat16)
    return skew(coefficients[:, ::-1], count_rows)


def filter_blocks(extended, fir, taps, length, block):
    tap_limit = fir.shape[1]
    channels = extended.shape[0]
    count = length // block
    main = extended[:, tap_limit - 1 :].reshape(channels, count, block)
    prefix = extended[:, :length].reshape(channels, count, block)[:, :, : tap_limit - 1]
    pieces = jnp.concatenate([prefix, main], axis=2)
    return jnp.einsum(
        "cnu,btu->bnct", pieces, band_matrix(fir, taps, block), preferred_element_type=jnp.float32
    )


def corr_kernel(off_ref, fw_ref, pp_ref, out_ref, acc_ref, *, chunks, groups, scale):
    acc_ref[...] = jnp.zeros_like(acc_ref)
    per = CHUNK // 128
    off = off_ref[0]

    def step(k, carry):
        first = k * per
        fa = jnp.concatenate([fw_ref[0, off + first + i] for i in range(per + 1)], axis=1)
        pa = jnp.concatenate([pp_ref[0, first + i] for i in range(per + 1)], axis=1)
        lhs = jnp.concatenate([fa[:, q : q + CHUNK] for q in range(SHIFTS)], axis=0)
        rhs = jnp.concatenate(
            [pa[:, 128 - g * SHIFTS : 128 - g * SHIFTS + CHUNK] for g in range(groups)], axis=0
        )
        acc_ref[...] += lax.dot_general(
            lhs, rhs, (((1,), (1,)), ((), ())), preferred_element_type=jnp.float32
        )
        return carry

    lax.fori_loop(0, chunks, step, 0)
    out_ref[0] = (acc_ref[...] * scale).astype(out_ref.dtype)


def correlate(offset, f_blocks, p_blocks, lags, chunks, scale):
    bands, nf, rows_f, _ = f_blocks.shape
    np_, rows_p = p_blocks.shape[1], p_blocks.shape[2]
    groups = lags // SHIFTS
    kernel = functools.partial(corr_kernel, chunks=chunks, groups=groups, scale=scale)
    m = SHIFTS * rows_f
    n = groups * rows_p
    grid_spec = pltpu.PrefetchScalarGridSpec(
        num_scalar_prefetch=1,
        grid=(bands,),
        in_specs=[
            pl.BlockSpec((1, nf, rows_f, 128), lambda b, o: (b, 0, 0, 0)),
            pl.BlockSpec((1, np_, rows_p, 128), lambda b, o: (b, 0, 0, 0)),
        ],
        out_specs=pl.BlockSpec((1, m, n), lambda b, o: (b, 0, 0)),
        scratch_shapes=[pltpu.VMEM((m, n), jnp.float32)],
    )
    return pl.pallas_call(
        kernel,
        grid_spec=grid_spec,
        out_shape=jax.ShapeDtypeStruct((bands, m, n), jnp.bfloat16),
        compiler_params=pltpu.CompilerParams(vmem_limit_bytes=48 * 1024 * 1024),
    )(offset, f_blocks, p_blocks)


def summed_over(value, axis):
    count = lax.axis_size(axis)
    bits = max(1, (count - 1).bit_length())
    rounds = [list(range(b, min(b + 2, bits))) for b in range(1, bits, 2)] + [[0]]
    for group in rounds:
        masks = [
            m for m in range(1, count)
            if all((m >> b) & 1 == 0 for b in range(bits) if b not in group)
        ]
        parts = [lax.ppermute(value, axis, [(i, i ^ m) for i in range(count)]) for m in masks]
        value = sum(parts, value)
    return value


def per_device(signal, fir, taps, sources):
    channels = signal.shape[0]
    tap_limit = fir.shape[1]
    shards = lax.axis_size("tm")
    samples_all = signal.shape[1] * shards
    lag_count = 2 * MAXLAG
    share = lag_count // shards
    norm_scale = samples_all ** (-0.5)
    groups = share // SHIFTS
    count_src = sources.shape[1]

    flat_src = sources.reshape(-1)
    local_ids = flat_src - lax.axis_index("sta") * channels
    onehot = (local_ids[:, None] == jnp.arange(channels, dtype=jnp.int32)[None, :]).astype(
        jnp.bfloat16
    )
    picks = jnp.dot(onehot, signal, preferred_element_type=jnp.float32).astype(jnp.bfloat16)
    picks = summed_over(picks, "sta")

    def filtered_of(rows):
        rows = lax.all_gather(rows, "tm", axis=1, tiled=True)
        extended = jnp.concatenate(
            [jnp.zeros((rows.shape[0], tap_limit - 1), rows.dtype), rows], axis=1
        )
        return filter_blocks(extended, fir, taps, samples_all, 128).astype(jnp.bfloat16)

    f_loc = filtered_of(signal)
    p_src = filtered_of(picks)

    span = samples_all + (groups - 1) * SHIFTS
    chunks = -(-span // CHUNK)
    blocks = chunks * CHUNK // 128 + 1
    data_blocks = samples_all // 128
    f_front = MAXLAG // 128
    f_blocks = jnp.pad(
        f_loc, ((0, 0), (f_front, blocks + lag_count // 128 - data_blocks - f_front), (0, 0), (0, 0))
    )
    p_blocks = jnp.pad(p_src, ((0, 0), (1, blocks - data_blocks - 1), (0, 0), (0, 0)))
    offset = (lax.axis_index("tm") * (share // 128)).astype(jnp.int32).reshape(1)

    out = correlate(offset, f_blocks, p_blocks, share, chunks, norm_scale)
    bands = out.shape[0]
    out = out.reshape(bands, SHIFTS, channels, groups, ROUNDS, count_src)
    out = jnp.transpose(out, (4, 0, 5, 2, 3, 1))
    return out.reshape(ROUNDS, bands, count_src, channels, share)


def solution(mesh):
    in_specs = (P("sta", "tm"), P(), P(), P())
    out_specs = P(None, None, None, "sta", "tm")
    return jax.shard_map(
        per_device, mesh=mesh, in_specs=in_specs, out_specs=out_specs, check_vma=False
    )
```

```python
import functools

import jax
import jax.numpy as jnp
from jax import lax
from jax.experimental import pallas as pl
from jax.experimental.pallas import tpu as pltpu
from jax.sharding import PartitionSpec as P

ROUNDS = 2
MAXLAG = 256
SHIFTS = 16
CHUNK = 2560


def skew(values, count_rows):
    leading = values.shape[:-1]
    length = values.shape[-1]
    row_width = length + count_rows
    padded = jnp.concatenate([values, jnp.zeros(leading + (count_rows,), values.dtype)], axis=-1)
    repeated = jnp.tile(padded, (1,) * len(leading) + (count_rows,))
    return repeated[..., : count_rows * (row_width - 1)].reshape(
        leading + (count_rows, row_width - 1)
    )


def band_matrix(fir, taps, count_rows):
    tap_limit = fir.shape[1]
    active = jnp.arange(tap_limit, dtype=jnp.int32)[None, :] < taps[:, None]
    coefficients = jnp.where(active, fir, 0.0).astype(jnp.bfloat16)
    return skew(coefficients[:, ::-1], count_rows)


def filter_blocks(extended, fir, taps, length, block):
    tap_limit = fir.shape[1]
    channels = extended.shape[0]
    count = length // block
    main = extended[:, tap_limit - 1 :].reshape(channels, count, block)
    prefix = extended[:, :length].reshape(channels, count, block)[:, :, : tap_limit - 1]
    pieces = jnp.concatenate([prefix, main], axis=2)
    return jnp.einsum(
        "cnu,btu->bnct", pieces, band_matrix(fir, taps, block), preferred_element_type=jnp.float32
    )


def corr_kernel(off_ref, fw_ref, pp_ref, out_ref, acc_ref, *, chunks, groups, scale):
    acc_ref[...] = jnp.zeros_like(acc_ref)
    per = CHUNK // 128
    off = off_ref[0]

    def step(k, carry):
        first = k * per
        fa = jnp.concatenate([fw_ref[0, off + first + i] for i in range(per + 1)], axis=1)
        pa = jnp.concatenate([pp_ref[0, first + i] for i in range(per + 1)], axis=1)
        lhs = jnp.concatenate([fa[:, q : q + CHUNK] for q in range(SHIFTS)], axis=0)
        rhs = jnp.concatenate(
            [pa[:, 128 - g * SHIFTS : 128 - g * SHIFTS + CHUNK] for g in range(groups)], axis=0
        )
        acc_ref[...] += lax.dot_general(
            lhs, rhs, (((1,), (1,)), ((), ())), preferred_element_type=jnp.float32
        )
        return carry

    lax.fori_loop(0, chunks, step, 0, unroll=True)
    out_ref[0] = (acc_ref[...] * scale).astype(out_ref.dtype)


def correlate(offset, f_blocks, p_blocks, lags, chunks, scale):
    bands, nf, rows_f, _ = f_blocks.shape
    np_, rows_p = p_blocks.shape[1], p_blocks.shape[2]
    groups = lags // SHIFTS
    kernel = functools.partial(corr_kernel, chunks=chunks, groups=groups, scale=scale)
    m = SHIFTS * rows_f
    n = groups * rows_p
    grid_spec = pltpu.PrefetchScalarGridSpec(
        num_scalar_prefetch=1,
        grid=(bands,),
        in_specs=[
            pl.BlockSpec((1, nf, rows_f, 128), lambda b, o: (b, 0, 0, 0)),
            pl.BlockSpec((1, np_, rows_p, 128), lambda b, o: (b, 0, 0, 0)),
        ],
        out_specs=pl.BlockSpec((1, m, n), lambda b, o: (b, 0, 0)),
        scratch_shapes=[pltpu.VMEM((m, n), jnp.float32)],
    )
    return pl.pallas_call(
        kernel,
        grid_spec=grid_spec,
        out_shape=jax.ShapeDtypeStruct((bands, m, n), jnp.bfloat16),
        compiler_params=pltpu.CompilerParams(vmem_limit_bytes=48 * 1024 * 1024),
    )(offset, f_blocks, p_blocks)


def summed_over(value, axis):
    count = lax.axis_size(axis)
    bits = max(1, (count - 1).bit_length())
    rounds = [list(range(b, min(b + 2, bits))) for b in range(1, bits, 2)] + [[0]]
    for group in rounds:
        masks = [
            m for m in range(1, count)
            if all((m >> b) & 1 == 0 for b in range(bits) if b not in group)
        ]
        parts = [lax.ppermute(value, axis, [(i, i ^ m) for i in range(count)]) for m in masks]
        value = sum(parts, value)
    return value


def per_device(signal, fir, taps, sources):
    channels = signal.shape[0]
    tap_limit = fir.shape[1]
    shards = lax.axis_size("tm")
    samples_all = signal.shape[1] * shards
    lag_count = 2 * MAXLAG
    share = lag_count // shards
    norm_scale = samples_all ** (-0.5)
    groups = share // SHIFTS
    count_src = sources.shape[1]

    flat_src = sources.reshape(-1)
    local_ids = flat_src - lax.axis_index("sta") * channels
    onehot = (local_ids[:, None] == jnp.arange(channels, dtype=jnp.int32)[None, :]).astype(
        jnp.bfloat16
    )
    picks = jnp.dot(onehot, signal, preferred_element_type=jnp.float32).astype(jnp.bfloat16)
    picks = summed_over(picks, "sta")

    def filtered_of(rows):
        rows = lax.all_gather(rows, "tm", axis=1, tiled=True)
        extended = jnp.concatenate(
            [jnp.zeros((rows.shape[0], tap_limit - 1), rows.dtype), rows], axis=1
        )
        return filter_blocks(extended, fir, taps, samples_all, 128).astype(jnp.bfloat16)

    f_loc = filtered_of(signal)
    p_src = filtered_of(picks)

    span = samples_all + (groups - 1) * SHIFTS
    chunks = -(-span // CHUNK)
    blocks = chunks * CHUNK // 128 + 1
    data_blocks = samples_all // 128
    f_front = MAXLAG // 128
    f_blocks = jnp.pad(
        f_loc, ((0, 0), (f_front, blocks + lag_count // 128 - data_blocks - f_front), (0, 0), (0, 0))
    )
    p_blocks = jnp.pad(p_src, ((0, 0), (1, blocks - data_blocks - 1), (0, 0), (0, 0)))
    offset = (lax.axis_index("tm") * (share // 128)).astype(jnp.int32).reshape(1)

    out = correlate(offset, f_blocks, p_blocks, share, chunks, norm_scale)
    bands = out.shape[0]
    out = out.reshape(bands, SHIFTS, channels, groups, ROUNDS, count_src)
    out = jnp.transpose(out, (4, 0, 5, 2, 3, 1))
    return out.reshape(ROUNDS, bands, count_src, channels, share)


def solution(mesh):
    in_specs = (P("sta", "tm"), P(), P(), P())
    out_specs = P(None, None, None, "sta", "tm")
    return jax.shard_map(
        per_device, mesh=mesh, in_specs=in_specs, out_specs=out_specs, check_vma=False
    )
```

```python
import functools

import jax
import jax.numpy as jnp
from jax import lax
from jax.experimental import pallas as pl
from jax.experimental.pallas import tpu as pltpu
from jax.sharding import PartitionSpec as P

ROUNDS = 2
MAXLAG = 256
SHIFTS = 16
CHUNK = 2560


def skew(values, count_rows):
    leading = values.shape[:-1]
    length = values.shape[-1]
    row_width = length + count_rows
    padded = jnp.concatenate([values, jnp.zeros(leading + (count_rows,), values.dtype)], axis=-1)
    repeated = jnp.tile(padded, (1,) * len(leading) + (count_rows,))
    return repeated[..., : count_rows * (row_width - 1)].reshape(
        leading + (count_rows, row_width - 1)
    )


def band_matrix(fir, taps, count_rows):
    tap_limit = fir.shape[1]
    active = jnp.arange(tap_limit, dtype=jnp.int32)[None, :] < taps[:, None]
    coefficients = jnp.where(active, fir, 0.0).astype(jnp.bfloat16)
    return skew(coefficients[:, ::-1], count_rows)


def filter_blocks(extended, fir, taps, length, block):
    tap_limit = fir.shape[1]
    channels = extended.shape[0]
    count = length // block
    main = extended[:, tap_limit - 1 :].reshape(channels, count, block)
    prefix = extended[:, :length].reshape(channels, count, block)[:, :, : tap_limit - 1]
    pieces = jnp.concatenate([prefix, main], axis=2)
    return jnp.einsum(
        "cnu,btu->bnct", pieces, band_matrix(fir, taps, block), preferred_element_type=jnp.float32
    )


def corr_kernel(off_ref, fw_ref, pp_ref, out_ref, acc_ref, *, chunks, groups, scale):
    acc_ref[...] = jnp.zeros_like(acc_ref)
    per = CHUNK // 128
    off = off_ref[0]

    def step(k, carry):
        first = k * per
        fa = jnp.concatenate([fw_ref[0, off + first + i] for i in range(per + 1)], axis=1)
        pa = jnp.concatenate([pp_ref[0, first + i] for i in range(per + 1)], axis=1)
        lhs = jnp.concatenate([fa[:, q : q + CHUNK] for q in range(SHIFTS)], axis=0)
        rhs = jnp.concatenate(
            [pa[:, 128 - g * SHIFTS : 128 - g * SHIFTS + CHUNK] for g in range(groups)], axis=0
        )
        acc_ref[...] += lax.dot_general(
            lhs, rhs, (((1,), (1,)), ((), ())), preferred_element_type=jnp.float32
        )
        return carry

    lax.fori_loop(0, chunks, step, 0, unroll=True)
    rounded = (acc_ref[...] * scale).astype(jnp.bfloat16)
    n = rounded.shape[1]
    rows_p = n // groups
    src = lax.broadcasted_iota(jnp.int32, (n, n), 0)
    dst = lax.broadcasted_iota(jnp.int32, (n, n), 1)
    perm = ((src % rows_p) * groups + src // rows_p == dst).astype(jnp.bfloat16)
    out_ref[0] = jnp.dot(rounded, perm, preferred_element_type=jnp.float32).astype(out_ref.dtype)


def correlate(offset, f_blocks, p_blocks, lags, chunks, scale):
    bands, nf, rows_f, _ = f_blocks.shape
    np_, rows_p = p_blocks.shape[1], p_blocks.shape[2]
    groups = lags // SHIFTS
    kernel = functools.partial(corr_kernel, chunks=chunks, groups=groups, scale=scale)
    m = SHIFTS * rows_f
    n = groups * rows_p
    grid_spec = pltpu.PrefetchScalarGridSpec(
        num_scalar_prefetch=1,
        grid=(bands,),
        in_specs=[
            pl.BlockSpec((1, nf, rows_f, 128), lambda b, o: (b, 0, 0, 0)),
            pl.BlockSpec((1, np_, rows_p, 128), lambda b, o: (b, 0, 0, 0)),
        ],
        out_specs=pl.BlockSpec((1, m, n), lambda b, o: (b, 0, 0)),
        scratch_shapes=[pltpu.VMEM((m, n), jnp.float32)],
    )
    return pl.pallas_call(
        kernel,
        grid_spec=grid_spec,
        out_shape=jax.ShapeDtypeStruct((bands, m, n), jnp.bfloat16),
        compiler_params=pltpu.CompilerParams(vmem_limit_bytes=48 * 1024 * 1024),
    )(offset, f_blocks, p_blocks)


def summed_over(value, axis):
    count = lax.axis_size(axis)
    bits = max(1, (count - 1).bit_length())
    rounds = [list(range(b, min(b + 2, bits))) for b in range(1, bits, 2)] + [[0]]
    for group in rounds:
        masks = [
            m for m in range(1, count)
            if all((m >> b) & 1 == 0 for b in range(bits) if b not in group)
        ]
        parts = [lax.ppermute(value, axis, [(i, i ^ m) for i in range(count)]) for m in masks]
        value = sum(parts, value)
    return value


def per_device(signal, fir, taps, sources):
    channels = signal.shape[0]
    tap_limit = fir.shape[1]
    shards = lax.axis_size("tm")
    samples_all = signal.shape[1] * shards
    lag_count = 2 * MAXLAG
    share = lag_count // shards
    norm_scale = samples_all ** (-0.5)
    groups = share // SHIFTS
    count_src = sources.shape[1]

    flat_src = sources.reshape(-1)
    local_ids = flat_src - lax.axis_index("sta") * channels
    onehot = (local_ids[:, None] == jnp.arange(channels, dtype=jnp.int32)[None, :]).astype(
        jnp.bfloat16
    )
    picks = jnp.dot(onehot, signal, preferred_element_type=jnp.float32).astype(jnp.bfloat16)
    picks = summed_over(picks, "sta")

    def filtered_of(rows):
        rows = lax.all_gather(rows, "tm", axis=1, tiled=True)
        extended = jnp.concatenate(
            [jnp.zeros((rows.shape[0], tap_limit - 1), rows.dtype), rows], axis=1
        )
        return filter_blocks(extended, fir, taps, samples_all, 128).astype(jnp.bfloat16)

    f_loc = filtered_of(signal)
    p_src = filtered_of(picks)

    span = samples_all + (groups - 1) * SHIFTS
    chunks = -(-span // CHUNK)
    blocks = chunks * CHUNK // 128 + 1
    data_blocks = samples_all // 128
    f_front = MAXLAG // 128
    f_blocks = jnp.pad(
        f_loc, ((0, 0), (f_front, blocks + lag_count // 128 - data_blocks - f_front), (0, 0), (0, 0))
    )
    p_blocks = jnp.pad(p_src, ((0, 0), (1, blocks - data_blocks - 1), (0, 0), (0, 0)))
    offset = (lax.axis_index("tm") * (share // 128)).astype(jnp.int32).reshape(1)

    out = correlate(offset, f_blocks, p_blocks, share, chunks, norm_scale)
    bands = out.shape[0]
    out = out.reshape(bands, SHIFTS, channels, ROUNDS, count_src, groups)
    out = jnp.transpose(out, (3, 0, 4, 2, 5, 1))
    return out.reshape(ROUNDS, bands, count_src, channels, share)


def solution(mesh):
    in_specs = (P("sta", "tm"), P(), P(), P())
    out_specs = P(None, None, None, "sta", "tm")
    return jax.shard_map(
        per_device, mesh=mesh, in_specs=in_specs, out_specs=out_specs, check_vma=False
    )
```

```python
import functools

import jax
import jax.numpy as jnp
from jax import lax
from jax.experimental import pallas as pl
from jax.experimental.pallas import tpu as pltpu
from jax.sharding import PartitionSpec as P

ROUNDS = 2
MAXLAG = 256
SHIFTS = 16
CHUNK = 3200


def skew(values, count_rows):
    leading = values.shape[:-1]
    length = values.shape[-1]
    row_width = length + count_rows
    padded = jnp.concatenate([values, jnp.zeros(leading + (count_rows,), values.dtype)], axis=-1)
    repeated = jnp.tile(padded, (1,) * len(leading) + (count_rows,))
    return repeated[..., : count_rows * (row_width - 1)].reshape(
        leading + (count_rows, row_width - 1)
    )


def band_matrix(fir, taps, count_rows):
    tap_limit = fir.shape[1]
    active = jnp.arange(tap_limit, dtype=jnp.int32)[None, :] < taps[:, None]
    coefficients = jnp.where(active, fir, 0.0).astype(jnp.bfloat16)
    return skew(coefficients[:, ::-1], count_rows)


def filter_blocks(extended, fir, taps, length, block):
    tap_limit = fir.shape[1]
    channels = extended.shape[0]
    count = length // block
    main = extended[:, tap_limit - 1 :].reshape(channels, count, block)
    prefix = extended[:, :length].reshape(channels, count, block)[:, :, : tap_limit - 1]
    pieces = jnp.concatenate([prefix, main], axis=2)
    return jnp.einsum(
        "cnu,btu->bnct", pieces, band_matrix(fir, taps, block), preferred_element_type=jnp.float32
    )


def corr_kernel(off_ref, fw_ref, pp_ref, out_ref, acc_ref, *, chunks, groups, scale):
    acc_ref[...] = jnp.zeros_like(acc_ref)
    per = CHUNK // 128
    off = off_ref[0]

    def step(k, carry):
        first = k * per
        fa = jnp.concatenate([fw_ref[0, off + first + i] for i in range(per + 1)], axis=1)
        pa = jnp.concatenate([pp_ref[0, first + i] for i in range(per + 1)], axis=1)
        lhs = jnp.concatenate([fa[:, q : q + CHUNK] for q in range(SHIFTS)], axis=0)
        rhs = jnp.concatenate(
            [pa[:, 128 - g * SHIFTS : 128 - g * SHIFTS + CHUNK] for g in range(groups)], axis=0
        )
        acc_ref[...] += lax.dot_general(
            lhs, rhs, (((1,), (1,)), ((), ())), preferred_element_type=jnp.float32
        )
        return carry

    lax.fori_loop(0, chunks, step, 0, unroll=True)
    rounded = (acc_ref[...] * scale).astype(jnp.bfloat16)
    n = rounded.shape[1]
    rows_p = n // groups
    src = lax.broadcasted_iota(jnp.int32, (n, n), 0)
    dst = lax.broadcasted_iota(jnp.int32, (n, n), 1)
    perm = ((src % rows_p) * groups + src // rows_p == dst).astype(jnp.bfloat16)
    out_ref[0] = jnp.dot(rounded, perm, preferred_element_type=jnp.float32).astype(out_ref.dtype)


def correlate(offset, f_blocks, p_blocks, lags, chunks, scale):
    bands, nf, rows_f, _ = f_blocks.shape
    np_, rows_p = p_blocks.shape[1], p_blocks.shape[2]
    groups = lags // SHIFTS
    kernel = functools.partial(corr_kernel, chunks=chunks, groups=groups, scale=scale)
    m = SHIFTS * rows_f
    n = groups * rows_p
    grid_spec = pltpu.PrefetchScalarGridSpec(
        num_scalar_prefetch=1,
        grid=(bands,),
        in_specs=[
            pl.BlockSpec((1, nf, rows_f, 128), lambda b, o: (b, 0, 0, 0)),
            pl.BlockSpec((1, np_, rows_p, 128), lambda b, o: (b, 0, 0, 0)),
        ],
        out_specs=pl.BlockSpec((1, m, n), lambda b, o: (b, 0, 0)),
        scratch_shapes=[pltpu.VMEM((m, n), jnp.float32)],
    )
    return pl.pallas_call(
        kernel,
        grid_spec=grid_spec,
        out_shape=jax.ShapeDtypeStruct((bands, m, n), jnp.bfloat16),
        compiler_params=pltpu.CompilerParams(vmem_limit_bytes=48 * 1024 * 1024),
    )(offset, f_blocks, p_blocks)


def summed_over(value, axis):
    count = lax.axis_size(axis)
    bits = max(1, (count - 1).bit_length())
    rounds = [list(range(b, min(b + 2, bits))) for b in range(1, bits, 2)] + [[0]]
    for group in rounds:
        masks = [
            m for m in range(1, count)
            if all((m >> b) & 1 == 0 for b in range(bits) if b not in group)
        ]
        parts = [lax.ppermute(value, axis, [(i, i ^ m) for i in range(count)]) for m in masks]
        value = sum(parts, value)
    return value


def per_device(signal, fir, taps, sources):
    channels = signal.shape[0]
    tap_limit = fir.shape[1]
    shards = lax.axis_size("tm")
    samples_all = signal.shape[1] * shards
    lag_count = 2 * MAXLAG
    share = lag_count // shards
    norm_scale = samples_all ** (-0.5)
    groups = share // SHIFTS
    count_src = sources.shape[1]

    flat_src = sources.reshape(-1)
    local_ids = flat_src - lax.axis_index("sta") * channels
    onehot = (local_ids[:, None] == jnp.arange(channels, dtype=jnp.int32)[None, :]).astype(
        jnp.bfloat16
    )
    picks = jnp.dot(onehot, signal, preferred_element_type=jnp.float32).astype(jnp.bfloat16)
    picks = summed_over(picks, "sta")

    def filtered_of(rows):
        rows = lax.all_gather(rows, "tm", axis=1, tiled=True)
        extended = jnp.concatenate(
            [jnp.zeros((rows.shape[0], tap_limit - 1), rows.dtype), rows], axis=1
        )
        return filter_blocks(extended, fir, taps, samples_all, 128).astype(jnp.bfloat16)

    f_loc = filtered_of(signal)
    p_src = filtered_of(picks)

    span = samples_all + (groups - 1) * SHIFTS
    chunks = -(-span // CHUNK)
    blocks = chunks * CHUNK // 128 + 1
    data_blocks = samples_all // 128
    f_front = MAXLAG // 128
    f_blocks = jnp.pad(
        f_loc, ((0, 0), (f_front, blocks + lag_count // 128 - data_blocks - f_front), (0, 0), (0, 0))
    )
    p_blocks = jnp.pad(p_src, ((0, 0), (1, blocks - data_blocks - 1), (0, 0), (0, 0)))
    offset = (lax.axis_index("tm") * (share // 128)).astype(jnp.int32).reshape(1)

    out = correlate(offset, f_blocks, p_blocks, share, chunks, norm_scale)
    bands = out.shape[0]
    out = out.reshape(bands, SHIFTS, channels, ROUNDS, count_src, groups)
    out = jnp.transpose(out, (3, 0, 4, 2, 5, 1))
    return out.reshape(ROUNDS, bands, count_src, channels, share)


def solution(mesh):
    in_specs = (P("sta", "tm"), P(), P(), P())
    out_specs = P(None, None, None, "sta", "tm")
    return jax.shard_map(
        per_device, mesh=mesh, in_specs=in_specs, out_specs=out_specs, check_vma=False
    )
```

```python
import functools

import jax
import jax.numpy as jnp
from jax import lax
from jax.experimental import pallas as pl
from jax.experimental.pallas import tpu as pltpu
from jax.sharding import PartitionSpec as P

ROUNDS = 2
MAXLAG = 256
SHIFTS = 16
CHUNK = 2560


def filter_in_blocks(rows, fir, taps):
    count, length = rows.shape
    tap_limit = fir.shape[1]
    blocks = jnp.transpose(rows.reshape(count, length // 128, 128), (1, 0, 2))
    before = jnp.pad(blocks[:-1], ((1, 0), (0, 0), (0, 0)))
    pieces = jnp.concatenate([before, blocks], axis=2)
    active = jnp.arange(tap_limit, dtype=jnp.int32)[None, :] < taps[:, None]
    coefficients = jnp.where(active, fir, 0.0).astype(jnp.bfloat16)
    lag = 128 + lax.broadcasted_iota(jnp.int32, (128, 256), 0) - lax.broadcasted_iota(
        jnp.int32, (128, 256), 1
    )
    inside = (lag >= 0) & (lag < tap_limit)
    banded = jnp.where(inside[None], coefficients[:, jnp.clip(lag, 0, tap_limit - 1)], 0.0)
    return jnp.einsum(
        "nru,btu->bnrt", pieces, banded.astype(jnp.bfloat16), preferred_element_type=jnp.float32
    )


def corr_kernel(off_ref, fw_ref, pp_ref, out_ref, acc_ref, *, chunks, groups, scale):
    acc_ref[...] = jnp.zeros_like(acc_ref)
    per = CHUNK // 128
    off = off_ref[0]

    def step(k, carry):
        first = k * per
        fa = jnp.concatenate([fw_ref[0, off + first + i] for i in range(per + 1)], axis=1)
        pa = jnp.concatenate([pp_ref[0, first + i] for i in range(per + 1)], axis=1)
        lhs = jnp.concatenate([fa[:, q : q + CHUNK] for q in range(SHIFTS)], axis=0)
        rhs = jnp.concatenate(
            [pa[:, 128 - g * SHIFTS : 128 - g * SHIFTS + CHUNK] for g in range(groups)], axis=0
        )
        acc_ref[...] += lax.dot_general(
            lhs, rhs, (((1,), (1,)), ((), ())), preferred_element_type=jnp.float32
        )
        return carry

    lax.fori_loop(0, chunks, step, 0, unroll=True)
    rounded = (acc_ref[...] * scale).astype(jnp.bfloat16)
    n = rounded.shape[1]
    rows_p = n // groups
    src = lax.broadcasted_iota(jnp.int32, (n, n), 0)
    dst = lax.broadcasted_iota(jnp.int32, (n, n), 1)
    perm = ((src % rows_p) * groups + src // rows_p == dst).astype(jnp.bfloat16)
    out_ref[0] = jnp.dot(rounded, perm, preferred_element_type=jnp.float32).astype(out_ref.dtype)


def correlate(offset, f_blocks, p_blocks, lags, chunks, scale):
    bands, nf, rows_f, _ = f_blocks.shape
    np_, rows_p = p_blocks.shape[1], p_blocks.shape[2]
    groups = lags // SHIFTS
    kernel = functools.partial(corr_kernel, chunks=chunks, groups=groups, scale=scale)
    m = SHIFTS * rows_f
    n = groups * rows_p
    grid_spec = pltpu.PrefetchScalarGridSpec(
        num_scalar_prefetch=1,
        grid=(bands,),
        in_specs=[
            pl.BlockSpec((1, nf, rows_f, 128), lambda b, o: (b, 0, 0, 0)),
            pl.BlockSpec((1, np_, rows_p, 128), lambda b, o: (b, 0, 0, 0)),
        ],
        out_specs=pl.BlockSpec((1, m, n), lambda b, o: (b, 0, 0)),
        scratch_shapes=[pltpu.VMEM((m, n), jnp.float32)],
    )
    return pl.pallas_call(
        kernel,
        grid_spec=grid_spec,
        out_shape=jax.ShapeDtypeStruct((bands, m, n), jnp.bfloat16),
        compiler_params=pltpu.CompilerParams(vmem_limit_bytes=48 * 1024 * 1024),
    )(offset, f_blocks, p_blocks)


def summed_over(value, axis):
    count = lax.axis_size(axis)
    bits = max(1, (count - 1).bit_length())
    rounds = [list(range(b, min(b + 2, bits))) for b in range(1, bits, 2)] + [[0]]
    for group in rounds:
        masks = [
            m for m in range(1, count)
            if all((m >> b) & 1 == 0 for b in range(bits) if b not in group)
        ]
        parts = [lax.ppermute(value, axis, [(i, i ^ m) for i in range(count)]) for m in masks]
        value = sum(parts, value)
    return value


def per_device(signal, fir, taps, sources):
    channels = signal.shape[0]
    shards = lax.axis_size("tm")
    samples_all = signal.shape[1] * shards
    lag_count = 2 * MAXLAG
    share = lag_count // shards
    norm_scale = samples_all ** (-0.5)
    groups = share // SHIFTS
    count_src = sources.shape[1]

    flat_src = sources.reshape(-1)
    local_ids = flat_src - lax.axis_index("sta") * channels
    onehot = (local_ids[:, None] == jnp.arange(channels, dtype=jnp.int32)[None, :]).astype(
        jnp.bfloat16
    )
    picks = jnp.dot(onehot, signal, preferred_element_type=jnp.float32).astype(jnp.bfloat16)
    picks = summed_over(picks, "sta")

    def filtered_of(rows):
        rows = lax.all_gather(rows, "tm", axis=1, tiled=True)
        return filter_in_blocks(rows, fir, taps).astype(jnp.bfloat16)

    f_loc = filtered_of(signal)
    p_src = filtered_of(picks)

    span = samples_all + (groups - 1) * SHIFTS
    chunks = -(-span // CHUNK)
    blocks = chunks * CHUNK // 128 + 1
    data_blocks = samples_all // 128
    f_front = MAXLAG // 128
    f_blocks = jnp.pad(
        f_loc, ((0, 0), (f_front, blocks + lag_count // 128 - data_blocks - f_front), (0, 0), (0, 0))
    )
    p_blocks = jnp.pad(p_src, ((0, 0), (1, blocks - data_blocks - 1), (0, 0), (0, 0)))
    offset = (lax.axis_index("tm") * (share // 128)).astype(jnp.int32).reshape(1)

    out = correlate(offset, f_blocks, p_blocks, share, chunks, norm_scale)
    bands = out.shape[0]
    out = out.reshape(bands, SHIFTS, channels, ROUNDS, count_src, groups)
    out = jnp.transpose(out, (3, 0, 4, 2, 5, 1))
    return out.reshape(ROUNDS, bands, count_src, channels, share)


def solution(mesh):
    in_specs = (P("sta", "tm"), P(), P(), P())
    out_specs = P(None, None, None, "sta", "tm")
    return jax.shard_map(
        per_device, mesh=mesh, in_specs=in_specs, out_specs=out_specs, check_vma=False
    )
```

```python
import functools

import jax
import jax.numpy as jnp
from jax import lax
from jax.experimental import pallas as pl
from jax.experimental.pallas import tpu as pltpu
from jax.sharding import PartitionSpec as P

ROUNDS = 2
MAXLAG = 256
SHIFTS = 16
CHUNK = 2560


def skew(values, count_rows):
    leading = values.shape[:-1]
    length = values.shape[-1]
    row_width = length + count_rows
    padded = jnp.concatenate([values, jnp.zeros(leading + (count_rows,), values.dtype)], axis=-1)
    repeated = jnp.tile(padded, (1,) * len(leading) + (count_rows,))
    return repeated[..., : count_rows * (row_width - 1)].reshape(
        leading + (count_rows, row_width - 1)
    )


def band_matrix(fir, taps, count_rows):
    tap_limit = fir.shape[1]
    active = jnp.arange(tap_limit, dtype=jnp.int32)[None, :] < taps[:, None]
    coefficients = jnp.where(active, fir, 0.0).astype(jnp.bfloat16)
    return skew(coefficients[:, ::-1], count_rows)


def filter_in_blocks(rows, fir, taps):
    count, length = rows.shape
    tap_limit = fir.shape[1]
    blocks = jnp.transpose(rows.reshape(count, length // 128, 128), (1, 0, 2))
    before = jnp.pad(blocks[:-1], ((1, 0), (0, 0), (0, 0)))
    pieces = jnp.concatenate([before, blocks], axis=2)
    banded = jnp.pad(band_matrix(fir, taps, 128), ((0, 0), (0, 0), (129 - tap_limit, 0)))
    return jnp.einsum(
        "nru,btu->bnrt", pieces, banded, preferred_element_type=jnp.float32
    )


def corr_kernel(off_ref, fw_ref, pp_ref, out_ref, acc_ref, *, chunks, groups, scale):
    acc_ref[...] = jnp.zeros_like(acc_ref)
    per = CHUNK // 128
    off = off_ref[0]

    def step(k, carry):
        first = k * per
        fa = jnp.concatenate([fw_ref[0, off + first + i] for i in range(per + 1)], axis=1)
        pa = jnp.concatenate([pp_ref[0, first + i] for i in range(per + 1)], axis=1)
        lhs = jnp.concatenate([fa[:, q : q + CHUNK] for q in range(SHIFTS)], axis=0)
        rhs = jnp.concatenate(
            [pa[:, 128 - g * SHIFTS : 128 - g * SHIFTS + CHUNK] for g in range(groups)], axis=0
        )
        acc_ref[...] += lax.dot_general(
            lhs, rhs, (((1,), (1,)), ((), ())), preferred_element_type=jnp.float32
        )
        return carry

    lax.fori_loop(0, chunks, step, 0, unroll=True)
    rounded = (acc_ref[...] * scale).astype(jnp.bfloat16)
    n = rounded.shape[1]
    rows_p = n // groups
    src = lax.broadcasted_iota(jnp.int32, (n, n), 0)
    dst = lax.broadcasted_iota(jnp.int32, (n, n), 1)
    perm = ((src % rows_p) * groups + src // rows_p == dst).astype(jnp.bfloat16)
    out_ref[0] = jnp.dot(rounded, perm, preferred_element_type=jnp.float32).astype(out_ref.dtype)


def correlate(offset, f_blocks, p_blocks, lags, chunks, scale):
    bands, nf, rows_f, _ = f_blocks.shape
    np_, rows_p = p_blocks.shape[1], p_blocks.shape[2]
    groups = lags // SHIFTS
    kernel = functools.partial(corr_kernel, chunks=chunks, groups=groups, scale=scale)
    m = SHIFTS * rows_f
    n = groups * rows_p
    grid_spec = pltpu.PrefetchScalarGridSpec(
        num_scalar_prefetch=1,
        grid=(bands,),
        in_specs=[
            pl.BlockSpec((1, nf, rows_f, 128), lambda b, o: (b, 0, 0, 0)),
            pl.BlockSpec((1, np_, rows_p, 128), lambda b, o: (b, 0, 0, 0)),
        ],
        out_specs=pl.BlockSpec((1, m, n), lambda b, o: (b, 0, 0)),
        scratch_shapes=[pltpu.VMEM((m, n), jnp.float32)],
    )
    return pl.pallas_call(
        kernel,
        grid_spec=grid_spec,
        out_shape=jax.ShapeDtypeStruct((bands, m, n), jnp.bfloat16),
        compiler_params=pltpu.CompilerParams(vmem_limit_bytes=48 * 1024 * 1024),
    )(offset, f_blocks, p_blocks)


def summed_over(value, axis):
    count = lax.axis_size(axis)
    bits = max(1, (count - 1).bit_length())
    rounds = [list(range(b, min(b + 2, bits))) for b in range(1, bits, 2)] + [[0]]
    for group in rounds:
        masks = [
            m for m in range(1, count)
            if all((m >> b) & 1 == 0 for b in range(bits) if b not in group)
        ]
        parts = [lax.ppermute(value, axis, [(i, i ^ m) for i in range(count)]) for m in masks]
        value = sum(parts, value)
    return value


def per_device(signal, fir, taps, sources):
    channels = signal.shape[0]
    shards = lax.axis_size("tm")
    samples_all = signal.shape[1] * shards
    lag_count = 2 * MAXLAG
    share = lag_count // shards
    norm_scale = samples_all ** (-0.5)
    groups = share // SHIFTS
    count_src = sources.shape[1]

    flat_src = sources.reshape(-1)
    local_ids = flat_src - lax.axis_index("sta") * channels
    onehot = (local_ids[:, None] == jnp.arange(channels, dtype=jnp.int32)[None, :]).astype(
        jnp.bfloat16
    )
    picks = jnp.dot(onehot, signal, preferred_element_type=jnp.float32).astype(jnp.bfloat16)
    picks = summed_over(picks, "sta")

    def filtered_of(rows):
        rows = lax.all_gather(rows, "tm", axis=1, tiled=True)
        return filter_in_blocks(rows, fir, taps).astype(jnp.bfloat16)

    f_loc = filtered_of(signal)
    p_src = filtered_of(picks)

    span = samples_all + (groups - 1) * SHIFTS
    chunks = -(-span // CHUNK)
    blocks = chunks * CHUNK // 128 + 1
    data_blocks = samples_all // 128
    f_front = MAXLAG // 128
    f_blocks = jnp.pad(
        f_loc, ((0, 0), (f_front, blocks + lag_count // 128 - data_blocks - f_front), (0, 0), (0, 0))
    )
    p_blocks = jnp.pad(p_src, ((0, 0), (1, blocks - data_blocks - 1), (0, 0), (0, 0)))
    offset = (lax.axis_index("tm") * (share // 128)).astype(jnp.int32).reshape(1)

    out = correlate(offset, f_blocks, p_blocks, share, chunks, norm_scale)
    bands = out.shape[0]
    out = out.reshape(bands, SHIFTS, channels, ROUNDS, count_src, groups)
    out = jnp.transpose(out, (3, 0, 4, 2, 5, 1))
    return out.reshape(ROUNDS, bands, count_src, channels, share)


def solution(mesh):
    in_specs = (P("sta", "tm"), P(), P(), P())
    out_specs = P(None, None, None, "sta", "tm")
    return jax.shard_map(
        per_device, mesh=mesh, in_specs=in_specs, out_specs=out_specs, check_vma=False
    )
```

```python
import functools

import jax
import jax.numpy as jnp
from jax import lax
from jax.experimental import pallas as pl
from jax.experimental.pallas import tpu as pltpu
from jax.sharding import PartitionSpec as P

ROUNDS = 2
MAXLAG = 256
SHIFTS = 16
CHUNK = 2560


def skew(values, count_rows):
    leading = values.shape[:-1]
    length = values.shape[-1]
    row_width = length + count_rows
    padded = jnp.concatenate([values, jnp.zeros(leading + (count_rows,), values.dtype)], axis=-1)
    repeated = jnp.tile(padded, (1,) * len(leading) + (count_rows,))
    return repeated[..., : count_rows * (row_width - 1)].reshape(
        leading + (count_rows, row_width - 1)
    )


def band_matrix(fir, taps, count_rows):
    tap_limit = fir.shape[1]
    active = jnp.arange(tap_limit, dtype=jnp.int32)[None, :] < taps[:, None]
    coefficients = jnp.where(active, fir, 0.0).astype(jnp.bfloat16)
    return skew(coefficients[:, ::-1], count_rows)


def filter_in_blocks(rows, fir, taps, front, back):
    count, length = rows.shape
    tap_limit = fir.shape[1]
    blocks = jnp.transpose(rows.reshape(count, length // 128, 128), (1, 0, 2))
    before = jnp.pad(blocks[:-1], ((1, 0), (0, 0), (0, 0)))
    pieces = jnp.concatenate([before, blocks], axis=2)
    pieces = jnp.pad(pieces, ((front, back), (0, 0), (0, 0)))
    banded = jnp.pad(band_matrix(fir, taps, 128), ((0, 0), (0, 0), (129 - tap_limit, 0)))
    return jnp.einsum(
        "nru,btu->bnrt", pieces, banded, preferred_element_type=jnp.float32
    )


def corr_kernel(off_ref, fw_ref, pp_ref, out_ref, acc_ref, *, chunks, groups, scale):
    acc_ref[...] = jnp.zeros_like(acc_ref)
    per = CHUNK // 128
    off = off_ref[0]

    def step(k, carry):
        first = k * per
        fa = jnp.concatenate([fw_ref[0, off + first + i] for i in range(per + 1)], axis=1)
        pa = jnp.concatenate([pp_ref[0, first + i] for i in range(per + 1)], axis=1)
        lhs = jnp.concatenate([fa[:, q : q + CHUNK] for q in range(SHIFTS)], axis=0)
        rhs = jnp.concatenate(
            [pa[:, 128 - g * SHIFTS : 128 - g * SHIFTS + CHUNK] for g in range(groups)], axis=0
        )
        acc_ref[...] += lax.dot_general(
            lhs, rhs, (((1,), (1,)), ((), ())), preferred_element_type=jnp.float32
        )
        return carry

    lax.fori_loop(0, chunks, step, 0, unroll=True)
    rounded = (acc_ref[...] * scale).astype(jnp.bfloat16)
    n = rounded.shape[1]
    rows_p = n // groups
    src = lax.broadcasted_iota(jnp.int32, (n, n), 0)
    dst = lax.broadcasted_iota(jnp.int32, (n, n), 1)
    perm = ((src % rows_p) * groups + src // rows_p == dst).astype(jnp.bfloat16)
    out_ref[0] = jnp.dot(rounded, perm, preferred_element_type=jnp.float32).astype(out_ref.dtype)


def correlate(offset, f_blocks, p_blocks, lags, chunks, scale):
    bands, nf, rows_f, _ = f_blocks.shape
    np_, rows_p = p_blocks.shape[1], p_blocks.shape[2]
    groups = lags // SHIFTS
    kernel = functools.partial(corr_kernel, chunks=chunks, groups=groups, scale=scale)
    m = SHIFTS * rows_f
    n = groups * rows_p
    grid_spec = pltpu.PrefetchScalarGridSpec(
        num_scalar_prefetch=1,
        grid=(bands,),
        in_specs=[
            pl.BlockSpec((1, nf, rows_f, 128), lambda b, o: (b, 0, 0, 0)),
            pl.BlockSpec((1, np_, rows_p, 128), lambda b, o: (b, 0, 0, 0)),
        ],
        out_specs=pl.BlockSpec((1, m, n), lambda b, o: (b, 0, 0)),
        scratch_shapes=[pltpu.VMEM((m, n), jnp.float32)],
    )
    return pl.pallas_call(
        kernel,
        grid_spec=grid_spec,
        out_shape=jax.ShapeDtypeStruct((bands, m, n), jnp.bfloat16),
        compiler_params=pltpu.CompilerParams(vmem_limit_bytes=48 * 1024 * 1024),
    )(offset, f_blocks, p_blocks)


def summed_over(value, axis):
    count = lax.axis_size(axis)
    bits = max(1, (count - 1).bit_length())
    rounds = [list(range(b, min(b + 2, bits))) for b in range(1, bits, 2)] + [[0]]
    for group in rounds:
        masks = [
            m for m in range(1, count)
            if all((m >> b) & 1 == 0 for b in range(bits) if b not in group)
        ]
        parts = [lax.ppermute(value, axis, [(i, i ^ m) for i in range(count)]) for m in masks]
        value = sum(parts, value)
    return value


def per_device(signal, fir, taps, sources):
    channels = signal.shape[0]
    shards = lax.axis_size("tm")
    samples_all = signal.shape[1] * shards
    lag_count = 2 * MAXLAG
    share = lag_count // shards
    norm_scale = samples_all ** (-0.5)
    groups = share // SHIFTS
    count_src = sources.shape[1]

    flat_src = sources.reshape(-1)
    local_ids = flat_src - lax.axis_index("sta") * channels
    onehot = (local_ids[:, None] == jnp.arange(channels, dtype=jnp.int32)[None, :]).astype(
        jnp.bfloat16
    )
    picks = jnp.dot(onehot, signal, preferred_element_type=jnp.float32).astype(jnp.bfloat16)
    picks = summed_over(picks, "sta")

    span = samples_all + (groups - 1) * SHIFTS
    chunks = -(-span // CHUNK)
    blocks = chunks * CHUNK // 128 + 1
    data_blocks = samples_all // 128
    f_front = MAXLAG // 128
    f_back = blocks + lag_count // 128 - data_blocks - f_front
    p_back = blocks - data_blocks - 1

    def filtered_of(rows, front, back):
        rows = lax.all_gather(rows, "tm", axis=1, tiled=True)
        return filter_in_blocks(rows, fir, taps, front, back).astype(jnp.bfloat16)

    f_blocks = filtered_of(signal, f_front, f_back)
    p_blocks = filtered_of(picks, 1, p_back)
    offset = (lax.axis_index("tm") * (share // 128)).astype(jnp.int32).reshape(1)

    out = correlate(offset, f_blocks, p_blocks, share, chunks, norm_scale)
    bands = out.shape[0]
    out = out.reshape(bands, SHIFTS, channels, ROUNDS, count_src, groups)
    out = jnp.transpose(out, (3, 0, 4, 2, 5, 1))
    return out.reshape(ROUNDS, bands, count_src, channels, share)


def solution(mesh):
    in_specs = (P("sta", "tm"), P(), P(), P())
    out_specs = P(None, None, None, "sta", "tm")
    return jax.shard_map(
        per_device, mesh=mesh, in_specs=in_specs, out_specs=out_specs, check_vma=False
    )
```

```python
import functools

import jax
import jax.numpy as jnp
from jax import lax
from jax.experimental import pallas as pl
from jax.experimental.pallas import tpu as pltpu
from jax.sharding import PartitionSpec as P

ROUNDS = 2
MAXLAG = 256
SHIFTS = 16
CHUNK = 2560


def skew(values, count_rows):
    leading = values.shape[:-1]
    length = values.shape[-1]
    row_width = length + count_rows
    padded = jnp.concatenate([values, jnp.zeros(leading + (count_rows,), values.dtype)], axis=-1)
    repeated = jnp.tile(padded, (1,) * len(leading) + (count_rows,))
    return repeated[..., : count_rows * (row_width - 1)].reshape(
        leading + (count_rows, row_width - 1)
    )


def band_matrix(fir, taps, count_rows):
    tap_limit = fir.shape[1]
    active = jnp.arange(tap_limit, dtype=jnp.int32)[None, :] < taps[:, None]
    coefficients = jnp.where(active, fir, 0.0).astype(jnp.bfloat16)
    return skew(coefficients[:, ::-1], count_rows)


def filter_in_blocks(rows, fir, taps):
    count, length = rows.shape
    tap_limit = fir.shape[1]
    blocks = jnp.transpose(rows.reshape(count, length // 128, 128), (1, 0, 2))
    before = jnp.pad(blocks[:-1], ((1, 0), (0, 0), (0, 0)))
    pieces = jnp.concatenate([before, blocks], axis=2)
    banded = jnp.pad(band_matrix(fir, taps, 128), ((0, 0), (0, 0), (129 - tap_limit, 0)))
    return jnp.einsum(
        "nru,btu->bnrt", pieces, banded, preferred_element_type=jnp.float32
    )


def corr_kernel(off_ref, fw_ref, pp_ref, out_ref, acc_ref, *, chunks, groups, scale):
    acc_ref[...] = jnp.zeros_like(acc_ref)
    per = CHUNK // 128
    off = off_ref[0]

    def step(k, carry):
        first = k * per
        fa = jnp.concatenate([fw_ref[0, off + first + i] for i in range(per + 1)], axis=1)
        pa = jnp.concatenate([pp_ref[0, first + i] for i in range(per + 1)], axis=1)
        lhs = jnp.concatenate([fa[:, q : q + CHUNK] for q in range(SHIFTS)], axis=0)
        rhs = jnp.concatenate(
            [pa[:, 128 - g * SHIFTS : 128 - g * SHIFTS + CHUNK] for g in range(groups)], axis=0
        )
        acc_ref[...] += lax.dot_general(
            lhs, rhs, (((1,), (1,)), ((), ())), preferred_element_type=jnp.float32
        )
        return carry

    lax.fori_loop(0, chunks, step, 0, unroll=True)
    rounded = (acc_ref[...] * scale).astype(jnp.bfloat16)
    n = rounded.shape[1]
    rows_p = n // groups
    src = lax.broadcasted_iota(jnp.int32, (n, n), 0)
    dst = lax.broadcasted_iota(jnp.int32, (n, n), 1)
    perm = ((src % rows_p) * groups + src // rows_p == dst).astype(jnp.bfloat16)
    out_ref[0] = jnp.dot(rounded, perm, preferred_element_type=jnp.float32).astype(out_ref.dtype)


def correlate(offset, f_blocks, p_blocks, lags, chunks, scale):
    bands, nf, rows_f, _ = f_blocks.shape
    np_, rows_p = p_blocks.shape[1], p_blocks.shape[2]
    groups = lags // SHIFTS
    kernel = functools.partial(corr_kernel, chunks=chunks, groups=groups, scale=scale)
    m = SHIFTS * rows_f
    n = groups * rows_p
    grid_spec = pltpu.PrefetchScalarGridSpec(
        num_scalar_prefetch=1,
        grid=(bands,),
        in_specs=[
            pl.BlockSpec((1, nf, rows_f, 128), lambda b, o: (b, 0, 0, 0)),
            pl.BlockSpec((1, np_, rows_p, 128), lambda b, o: (b, 0, 0, 0)),
        ],
        out_specs=pl.BlockSpec((1, m, n), lambda b, o: (b, 0, 0)),
        scratch_shapes=[pltpu.VMEM((m, n), jnp.float32)],
    )
    return pl.pallas_call(
        kernel,
        grid_spec=grid_spec,
        out_shape=jax.ShapeDtypeStruct((bands, m, n), jnp.bfloat16),
        compiler_params=pltpu.CompilerParams(vmem_limit_bytes=48 * 1024 * 1024),
    )(offset, f_blocks, p_blocks)


def summed_over(value, axis, companion):
    count = lax.axis_size(axis)
    bits = max(1, (count - 1).bit_length())
    rounds = [list(range(b, min(b + 2, bits))) for b in range(1, bits, 2)] + [[0]]
    for index, group in enumerate(rounds):
        masks = [
            m for m in range(1, count)
            if all((m >> b) & 1 == 0 for b in range(bits) if b not in group)
        ]
        parts = [lax.ppermute(value, axis, [(i, i ^ m) for i in range(count)]) for m in masks]
        value = sum(parts, value)
        if index == 0:
            value, companion = lax.optimization_barrier((value, companion))
    return value, companion


def per_device(signal, fir, taps, sources):
    channels = signal.shape[0]
    shards = lax.axis_size("tm")
    samples_all = signal.shape[1] * shards
    lag_count = 2 * MAXLAG
    share = lag_count // shards
    norm_scale = samples_all ** (-0.5)
    groups = share // SHIFTS
    count_src = sources.shape[1]

    flat_src = sources.reshape(-1)
    local_ids = flat_src - lax.axis_index("sta") * channels
    onehot = (local_ids[:, None] == jnp.arange(channels, dtype=jnp.int32)[None, :]).astype(
        jnp.bfloat16
    )
    picks = jnp.dot(onehot, signal, preferred_element_type=jnp.float32).astype(jnp.bfloat16)
    picks, signal = summed_over(picks, "sta", signal)

    def filtered_of(rows):
        rows = lax.all_gather(rows, "tm", axis=1, tiled=True)
        return filter_in_blocks(rows, fir, taps).astype(jnp.bfloat16)

    f_loc = filtered_of(signal)
    p_src = filtered_of(picks)

    span = samples_all + (groups - 1) * SHIFTS
    chunks = -(-span // CHUNK)
    blocks = chunks * CHUNK // 128 + 1
    data_blocks = samples_all // 128
    f_front = MAXLAG // 128
    f_blocks = jnp.pad(
        f_loc, ((0, 0), (f_front, blocks + lag_count // 128 - data_blocks - f_front), (0, 0), (0, 0))
    )
    p_blocks = jnp.pad(p_src, ((0, 0), (1, blocks - data_blocks - 1), (0, 0), (0, 0)))
    offset = (lax.axis_index("tm") * (share // 128)).astype(jnp.int32).reshape(1)

    out = correlate(offset, f_blocks, p_blocks, share, chunks, norm_scale)
    bands = out.shape[0]
    out = out.reshape(bands, SHIFTS, channels, ROUNDS, count_src, groups)
    out = jnp.transpose(out, (3, 0, 4, 2, 5, 1))
    return out.reshape(ROUNDS, bands, count_src, channels, share)


def solution(mesh):
    in_specs = (P("sta", "tm"), P(), P(), P())
    out_specs = P(None, None, None, "sta", "tm")
    return jax.shard_map(
        per_device, mesh=mesh, in_specs=in_specs, out_specs=out_specs, check_vma=False
    )
```

```python
import functools

import jax
import jax.numpy as jnp
from jax import lax
from jax.experimental import pallas as pl
from jax.experimental.pallas import tpu as pltpu
from jax.sharding import PartitionSpec as P

ROUNDS = 2
MAXLAG = 256
SHIFTS = 16
CHUNK = 2560


def skew(values, count_rows):
    leading = values.shape[:-1]
    length = values.shape[-1]
    row_width = length + count_rows
    padded = jnp.concatenate([values, jnp.zeros(leading + (count_rows,), values.dtype)], axis=-1)
    repeated = jnp.tile(padded, (1,) * len(leading) + (count_rows,))
    return repeated[..., : count_rows * (row_width - 1)].reshape(
        leading + (count_rows, row_width - 1)
    )


def band_matrix(fir, taps, count_rows):
    tap_limit = fir.shape[1]
    active = jnp.arange(tap_limit, dtype=jnp.int32)[None, :] < taps[:, None]
    coefficients = jnp.where(active, fir, 0.0).astype(jnp.bfloat16)
    return skew(coefficients[:, ::-1], count_rows)


def filter_in_blocks(rows, fir, taps):
    count, length = rows.shape
    tap_limit = fir.shape[1]
    blocks = jnp.transpose(rows.reshape(count, length // 128, 128), (1, 0, 2))
    before = jnp.pad(blocks[:-1], ((1, 0), (0, 0), (0, 0)))
    pieces = jnp.concatenate([before, blocks], axis=2)
    banded = jnp.pad(band_matrix(fir, taps, 128), ((0, 0), (0, 0), (129 - tap_limit, 0)))
    return jnp.einsum(
        "nru,btu->bnrt", pieces, banded, preferred_element_type=jnp.float32
    )


def corr_kernel(off_ref, fw_ref, pp_ref, out_ref, acc_ref, *, chunks, groups, scale):
    acc_ref[...] = jnp.zeros_like(acc_ref)
    per = CHUNK // 128
    off = off_ref[0]

    def step(k, carry):
        first = k * per
        fa = jnp.concatenate([fw_ref[0, off + first + i] for i in range(per + 1)], axis=1)
        pa = jnp.concatenate([pp_ref[0, first + i] for i in range(per + 1)], axis=1)
        lhs = jnp.concatenate([fa[:, q : q + CHUNK] for q in range(SHIFTS)], axis=0)
        rhs = jnp.concatenate(
            [pa[:, 128 - g * SHIFTS : 128 - g * SHIFTS + CHUNK] for g in range(groups)], axis=0
        )
        acc_ref[...] += lax.dot_general(
            lhs, rhs, (((1,), (1,)), ((), ())), preferred_element_type=jnp.float32
        )
        return carry

    lax.fori_loop(0, chunks, step, 0, unroll=True)
    rounded = (acc_ref[...] * scale).astype(jnp.bfloat16)
    n = rounded.shape[1]
    rows_p = n // groups
    src = lax.broadcasted_iota(jnp.int32, (n, n), 0)
    dst = lax.broadcasted_iota(jnp.int32, (n, n), 1)
    perm = ((src % rows_p) * groups + src // rows_p == dst).astype(jnp.bfloat16)
    out_ref[0] = jnp.dot(rounded, perm, preferred_element_type=jnp.float32).astype(out_ref.dtype)


def correlate(offset, f_blocks, p_blocks, lags, chunks, scale):
    bands, nf, rows_f, _ = f_blocks.shape
    np_, rows_p = p_blocks.shape[1], p_blocks.shape[2]
    groups = lags // SHIFTS
    kernel = functools.partial(corr_kernel, chunks=chunks, groups=groups, scale=scale)
    m = SHIFTS * rows_f
    n = groups * rows_p
    grid_spec = pltpu.PrefetchScalarGridSpec(
        num_scalar_prefetch=1,
        grid=(bands,),
        in_specs=[
            pl.BlockSpec((1, nf, rows_f, 128), lambda b, o: (b, 0, 0, 0)),
            pl.BlockSpec((1, np_, rows_p, 128), lambda b, o: (b, 0, 0, 0)),
        ],
        out_specs=pl.BlockSpec((1, m, n), lambda b, o: (b, 0, 0)),
        scratch_shapes=[pltpu.VMEM((m, n), jnp.float32)],
    )
    return pl.pallas_call(
        kernel,
        grid_spec=grid_spec,
        out_shape=jax.ShapeDtypeStruct((bands, m, n), jnp.bfloat16),
        compiler_params=pltpu.CompilerParams(vmem_limit_bytes=48 * 1024 * 1024),
    )(offset, f_blocks, p_blocks)


def summed_over(value, axis):
    count = lax.axis_size(axis)
    bits = max(1, (count - 1).bit_length())
    rounds = [list(range(b, min(b + 2, bits))) for b in range(1, bits, 2)][::-1] + [[0]]
    for group in rounds:
        masks = [
            m for m in range(1, count)
            if all((m >> b) & 1 == 0 for b in range(bits) if b not in group)
        ]
        parts = [lax.ppermute(value, axis, [(i, i ^ m) for i in range(count)]) for m in masks]
        value = sum(parts, value)
    return value


def per_device(signal, fir, taps, sources):
    channels = signal.shape[0]
    shards = lax.axis_size("tm")
    samples_all = signal.shape[1] * shards
    lag_count = 2 * MAXLAG
    share = lag_count // shards
    norm_scale = samples_all ** (-0.5)
    groups = share // SHIFTS
    count_src = sources.shape[1]

    flat_src = sources.reshape(-1)
    local_ids = flat_src - lax.axis_index("sta") * channels
    onehot = (local_ids[:, None] == jnp.arange(channels, dtype=jnp.int32)[None, :]).astype(
        jnp.bfloat16
    )
    picks = jnp.dot(onehot, signal, preferred_element_type=jnp.float32).astype(jnp.bfloat16)
    picks = summed_over(picks, "sta")

    def filtered_of(rows):
        rows = lax.all_gather(rows, "tm", axis=1, tiled=True)
        return filter_in_blocks(rows, fir, taps).astype(jnp.bfloat16)

    f_loc = filtered_of(signal)
    p_src = filtered_of(picks)

    span = samples_all + (groups - 1) * SHIFTS
    chunks = -(-span // CHUNK)
    blocks = chunks * CHUNK // 128 + 1
    data_blocks = samples_all // 128
    f_front = MAXLAG // 128
    f_blocks = jnp.pad(
        f_loc, ((0, 0), (f_front, blocks + lag_count // 128 - data_blocks - f_front), (0, 0), (0, 0))
    )
    p_blocks = jnp.pad(p_src, ((0, 0), (1, blocks - data_blocks - 1), (0, 0), (0, 0)))
    offset = (lax.axis_index("tm") * (share // 128)).astype(jnp.int32).reshape(1)

    out = correlate(offset, f_blocks, p_blocks, share, chunks, norm_scale)
    bands = out.shape[0]
    out = out.reshape(bands, SHIFTS, channels, ROUNDS, count_src, groups)
    out = jnp.transpose(out, (3, 0, 4, 2, 5, 1))
    return out.reshape(ROUNDS, bands, count_src, channels, share)


def solution(mesh):
    in_specs = (P("sta", "tm"), P(), P(), P())
    out_specs = P(None, None, None, "sta", "tm")
    return jax.shard_map(
        per_device, mesh=mesh, in_specs=in_specs, out_specs=out_specs, check_vma=False
    )
```

```python
import functools

import jax
import jax.numpy as jnp
from jax import lax
from jax.experimental import pallas as pl
from jax.experimental.pallas import tpu as pltpu
from jax.sharding import PartitionSpec as P

ROUNDS = 2
MAXLAG = 256
SHIFTS = 16
CHUNK = 2560


def skew(values, count_rows):
    leading = values.shape[:-1]
    length = values.shape[-1]
    row_width = length + count_rows
    padded = jnp.concatenate([values, jnp.zeros(leading + (count_rows,), values.dtype)], axis=-1)
    repeated = jnp.tile(padded, (1,) * len(leading) + (count_rows,))
    return repeated[..., : count_rows * (row_width - 1)].reshape(
        leading + (count_rows, row_width - 1)
    )


def band_matrix(fir, taps, count_rows):
    tap_limit = fir.shape[1]
    active = jnp.arange(tap_limit, dtype=jnp.int32)[None, :] < taps[:, None]
    coefficients = jnp.where(active, fir, 0.0).astype(jnp.bfloat16)
    return skew(coefficients[:, ::-1], count_rows)


def filter_in_blocks(rows, fir, taps):
    count, length = rows.shape
    tap_limit = fir.shape[1]
    blocks = jnp.transpose(rows.reshape(count, length // 128, 128), (1, 0, 2))
    before = jnp.pad(blocks[:-1], ((1, 0), (0, 0), (0, 0)))
    pieces = jnp.concatenate([before, blocks], axis=2)
    banded = jnp.pad(band_matrix(fir, taps, 128), ((0, 0), (0, 0), (129 - tap_limit, 0)))
    return jnp.einsum(
        "nru,btu->bnrt", pieces, banded, preferred_element_type=jnp.float32
    )


def corr_kernel(off_ref, fw_ref, pp_ref, out_ref, acc_ref, *, widths, groups, scale):
    acc_ref[...] = jnp.zeros_like(acc_ref)
    off = off_ref[0]
    first = 0
    for width in widths:
        per = width // 128
        fa = jnp.concatenate([fw_ref[0, off + first + i] for i in range(per + 1)], axis=1)
        pa = jnp.concatenate([pp_ref[0, first + i] for i in range(per + 1)], axis=1)
        lhs = jnp.concatenate([fa[:, q : q + width] for q in range(SHIFTS)], axis=0)
        rhs = jnp.concatenate(
            [pa[:, 128 - g * SHIFTS : 128 - g * SHIFTS + width] for g in range(groups)], axis=0
        )
        acc_ref[...] += lax.dot_general(
            lhs, rhs, (((1,), (1,)), ((), ())), preferred_element_type=jnp.float32
        )
        first += per

    rounded = (acc_ref[...] * scale).astype(jnp.bfloat16)
    n = rounded.shape[1]
    rows_p = n // groups
    src = lax.broadcasted_iota(jnp.int32, (n, n), 0)
    dst = lax.broadcasted_iota(jnp.int32, (n, n), 1)
    perm = ((src % rows_p) * groups + src // rows_p == dst).astype(jnp.bfloat16)
    out_ref[0] = jnp.dot(rounded, perm, preferred_element_type=jnp.float32).astype(out_ref.dtype)


def correlate(offset, f_blocks, p_blocks, lags, chunks, scale, span):
    bands, nf, rows_f, _ = f_blocks.shape
    np_, rows_p = p_blocks.shape[1], p_blocks.shape[2]
    groups = lags // SHIFTS
    needed = -(-span // 128) * 128
    widths = tuple([CHUNK] * (chunks - 1) + [needed - (chunks - 1) * CHUNK])
    kernel = functools.partial(corr_kernel, widths=widths, groups=groups, scale=scale)
    m = SHIFTS * rows_f
    n = groups * rows_p
    grid_spec = pltpu.PrefetchScalarGridSpec(
        num_scalar_prefetch=1,
        grid=(bands,),
        in_specs=[
            pl.BlockSpec((1, nf, rows_f, 128), lambda b, o: (b, 0, 0, 0)),
            pl.BlockSpec((1, np_, rows_p, 128), lambda b, o: (b, 0, 0, 0)),
        ],
        out_specs=pl.BlockSpec((1, m, n), lambda b, o: (b, 0, 0)),
        scratch_shapes=[pltpu.VMEM((m, n), jnp.float32)],
    )
    return pl.pallas_call(
        kernel,
        grid_spec=grid_spec,
        out_shape=jax.ShapeDtypeStruct((bands, m, n), jnp.bfloat16),
        compiler_params=pltpu.CompilerParams(vmem_limit_bytes=48 * 1024 * 1024),
    )(offset, f_blocks, p_blocks)


def summed_over(value, axis):
    count = lax.axis_size(axis)
    bits = max(1, (count - 1).bit_length())
    rounds = [list(range(b, min(b + 2, bits))) for b in range(1, bits, 2)][::-1] + [[0]]
    for group in rounds:
        masks = [
            m for m in range(1, count)
            if all((m >> b) & 1 == 0 for b in range(bits) if b not in group)
        ]
        parts = [lax.ppermute(value, axis, [(i, i ^ m) for i in range(count)]) for m in masks]
        value = sum(parts, value)
    return value


def per_device(signal, fir, taps, sources):
    channels = signal.shape[0]
    shards = lax.axis_size("tm")
    samples_all = signal.shape[1] * shards
    lag_count = 2 * MAXLAG
    share = lag_count // shards
    norm_scale = samples_all ** (-0.5)
    groups = share // SHIFTS
    count_src = sources.shape[1]

    flat_src = sources.reshape(-1)
    local_ids = flat_src - lax.axis_index("sta") * channels
    onehot = (local_ids[:, None] == jnp.arange(channels, dtype=jnp.int32)[None, :]).astype(
        jnp.bfloat16
    )
    picks = jnp.dot(onehot, signal, preferred_element_type=jnp.float32).astype(jnp.bfloat16)
    picks = summed_over(picks, "sta")

    def filtered_of(rows):
        rows = lax.all_gather(rows, "tm", axis=1, tiled=True)
        return filter_in_blocks(rows, fir, taps).astype(jnp.bfloat16)

    f_loc = filtered_of(signal)
    p_src = filtered_of(picks)

    span = samples_all + (groups - 1) * SHIFTS
    chunks = -(-span // CHUNK)
    blocks = chunks * CHUNK // 128 + 1
    data_blocks = samples_all // 128
    f_front = MAXLAG // 128
    f_blocks = jnp.pad(
        f_loc, ((0, 0), (f_front, blocks + lag_count // 128 - data_blocks - f_front), (0, 0), (0, 0))
    )
    p_blocks = jnp.pad(p_src, ((0, 0), (1, blocks - data_blocks - 1), (0, 0), (0, 0)))
    offset = (lax.axis_index("tm") * (share // 128)).astype(jnp.int32).reshape(1)

    out = correlate(offset, f_blocks, p_blocks, share, chunks, norm_scale, span)
    bands = out.shape[0]
    out = out.reshape(bands, SHIFTS, channels, ROUNDS, count_src, groups)
    out = jnp.transpose(out, (3, 0, 4, 2, 5, 1))
    return out.reshape(ROUNDS, bands, count_src, channels, share)


def solution(mesh):
    in_specs = (P("sta", "tm"), P(), P(), P())
    out_specs = P(None, None, None, "sta", "tm")
    return jax.shard_map(
        per_device, mesh=mesh, in_specs=in_specs, out_specs=out_specs, check_vma=False
    )
```

```python
import functools

import jax
import jax.numpy as jnp
from jax import lax
from jax.experimental import pallas as pl
from jax.experimental.pallas import tpu as pltpu
from jax.sharding import PartitionSpec as P

ROUNDS = 2
MAXLAG = 256
SHIFTS = 16
CHUNK = 3200


def skew(values, count_rows):
    leading = values.shape[:-1]
    length = values.shape[-1]
    row_width = length + count_rows
    padded = jnp.concatenate([values, jnp.zeros(leading + (count_rows,), values.dtype)], axis=-1)
    repeated = jnp.tile(padded, (1,) * len(leading) + (count_rows,))
    return repeated[..., : count_rows * (row_width - 1)].reshape(
        leading + (count_rows, row_width - 1)
    )


def band_matrix(fir, taps, count_rows):
    tap_limit = fir.shape[1]
    active = jnp.arange(tap_limit, dtype=jnp.int32)[None, :] < taps[:, None]
    coefficients = jnp.where(active, fir, 0.0).astype(jnp.bfloat16)
    return skew(coefficients[:, ::-1], count_rows)


def filter_in_blocks(rows, fir, taps):
    count, length = rows.shape
    tap_limit = fir.shape[1]
    blocks = jnp.transpose(rows.reshape(count, length // 128, 128), (1, 0, 2))
    before = jnp.pad(blocks[:-1], ((1, 0), (0, 0), (0, 0)))
    pieces = jnp.concatenate([before, blocks], axis=2)
    banded = jnp.pad(band_matrix(fir, taps, 128), ((0, 0), (0, 0), (129 - tap_limit, 0)))
    return jnp.einsum(
        "nru,btu->bnrt", pieces, banded, preferred_element_type=jnp.float32
    )


def corr_kernel(off_ref, fw_ref, pp_ref, out_ref, acc_ref, *, widths, groups, scale):
    acc_ref[...] = jnp.zeros_like(acc_ref)
    off = off_ref[0]
    first = 0
    for width in widths:
        per = width // 128
        fa = jnp.concatenate([fw_ref[0, off + first + i] for i in range(per + 1)], axis=1)
        pa = jnp.concatenate([pp_ref[0, first + i] for i in range(per + 1)], axis=1)
        lhs = jnp.concatenate([fa[:, q : q + width] for q in range(SHIFTS)], axis=0)
        rhs = jnp.concatenate(
            [pa[:, 128 - g * SHIFTS : 128 - g * SHIFTS + width] for g in range(groups)], axis=0
        )
        acc_ref[...] += lax.dot_general(
            lhs, rhs, (((1,), (1,)), ((), ())), preferred_element_type=jnp.float32
        )
        first += per

    rounded = (acc_ref[...] * scale).astype(jnp.bfloat16)
    n = rounded.shape[1]
    rows_p = n // groups
    src = lax.broadcasted_iota(jnp.int32, (n, n), 0)
    dst = lax.broadcasted_iota(jnp.int32, (n, n), 1)
    perm = ((src % rows_p) * groups + src // rows_p == dst).astype(jnp.bfloat16)
    out_ref[0] = jnp.dot(rounded, perm, preferred_element_type=jnp.float32).astype(out_ref.dtype)


def correlate(offset, f_blocks, p_blocks, lags, chunks, scale, span):
    bands, nf, rows_f, _ = f_blocks.shape
    np_, rows_p = p_blocks.shape[1], p_blocks.shape[2]
    groups = lags // SHIFTS
    needed = -(-span // 128)
    base, extra = divmod(needed, chunks)
    widths = tuple((base + (i >= chunks - extra)) * 128 for i in range(chunks))
    kernel = functools.partial(corr_kernel, widths=widths, groups=groups, scale=scale)
    m = SHIFTS * rows_f
    n = groups * rows_p
    grid_spec = pltpu.PrefetchScalarGridSpec(
        num_scalar_prefetch=1,
        grid=(bands,),
        in_specs=[
            pl.BlockSpec((1, nf, rows_f, 128), lambda b, o: (b, 0, 0, 0)),
            pl.BlockSpec((1, np_, rows_p, 128), lambda b, o: (b, 0, 0, 0)),
        ],
        out_specs=pl.BlockSpec((1, m, n), lambda b, o: (b, 0, 0)),
        scratch_shapes=[pltpu.VMEM((m, n), jnp.float32)],
    )
    return pl.pallas_call(
        kernel,
        grid_spec=grid_spec,
        out_shape=jax.ShapeDtypeStruct((bands, m, n), jnp.bfloat16),
        compiler_params=pltpu.CompilerParams(vmem_limit_bytes=48 * 1024 * 1024),
    )(offset, f_blocks, p_blocks)


def summed_over(value, axis):
    count = lax.axis_size(axis)
    bits = max(1, (count - 1).bit_length())
    rounds = [list(range(b, min(b + 2, bits))) for b in range(1, bits, 2)][::-1] + [[0]]
    for group in rounds:
        masks = [
            m for m in range(1, count)
            if all((m >> b) & 1 == 0 for b in range(bits) if b not in group)
        ]
        parts = [lax.ppermute(value, axis, [(i, i ^ m) for i in range(count)]) for m in masks]
        value = sum(parts, value)
    return value


def per_device(signal, fir, taps, sources):
    channels = signal.shape[0]
    shards = lax.axis_size("tm")
    samples_all = signal.shape[1] * shards
    lag_count = 2 * MAXLAG
    share = lag_count // shards
    norm_scale = samples_all ** (-0.5)
    groups = share // SHIFTS
    count_src = sources.shape[1]

    flat_src = sources.reshape(-1)
    local_ids = flat_src - lax.axis_index("sta") * channels
    onehot = (local_ids[:, None] == jnp.arange(channels, dtype=jnp.int32)[None, :]).astype(
        jnp.bfloat16
    )
    picks = jnp.dot(onehot, signal, preferred_element_type=jnp.float32).astype(jnp.bfloat16)
    picks = summed_over(picks, "sta")

    def filtered_of(rows):
        rows = lax.all_gather(rows, "tm", axis=1, tiled=True)
        return filter_in_blocks(rows, fir, taps).astype(jnp.bfloat16)

    f_loc = filtered_of(signal)
    p_src = filtered_of(picks)

    span = samples_all + (groups - 1) * SHIFTS
    chunks = -(-span // CHUNK)
    blocks = chunks * CHUNK // 128 + 1
    data_blocks = samples_all // 128
    f_front = MAXLAG // 128
    f_blocks = jnp.pad(
        f_loc, ((0, 0), (f_front, blocks + lag_count // 128 - data_blocks - f_front), (0, 0), (0, 0))
    )
    p_blocks = jnp.pad(p_src, ((0, 0), (1, blocks - data_blocks - 1), (0, 0), (0, 0)))
    offset = (lax.axis_index("tm") * (share // 128)).astype(jnp.int32).reshape(1)

    out = correlate(offset, f_blocks, p_blocks, share, chunks, norm_scale, span)
    bands = out.shape[0]
    out = out.reshape(bands, SHIFTS, channels, ROUNDS, count_src, groups)
    out = jnp.transpose(out, (3, 0, 4, 2, 5, 1))
    return out.reshape(ROUNDS, bands, count_src, channels, share)


def solution(mesh):
    in_specs = (P("sta", "tm"), P(), P(), P())
    out_specs = P(None, None, None, "sta", "tm")
    return jax.shard_map(
        per_device, mesh=mesh, in_specs=in_specs, out_specs=out_specs, check_vma=False
    )
```

```python
import functools

import jax
import jax.numpy as jnp
from jax import lax
from jax.experimental import pallas as pl
from jax.experimental.pallas import tpu as pltpu
from jax.sharding import PartitionSpec as P

ROUNDS = 2
MAXLAG = 256
SHIFTS = 16
CHUNK = 3200
PAIR = 2


def skew(values, count_rows):
    leading = values.shape[:-1]
    length = values.shape[-1]
    row_width = length + count_rows
    padded = jnp.concatenate([values, jnp.zeros(leading + (count_rows,), values.dtype)], axis=-1)
    repeated = jnp.tile(padded, (1,) * len(leading) + (count_rows,))
    return repeated[..., : count_rows * (row_width - 1)].reshape(
        leading + (count_rows, row_width - 1)
    )


def band_matrix(fir, taps, count_rows):
    tap_limit = fir.shape[1]
    active = jnp.arange(tap_limit, dtype=jnp.int32)[None, :] < taps[:, None]
    coefficients = jnp.where(active, fir, 0.0).astype(jnp.bfloat16)
    return skew(coefficients[:, ::-1], count_rows)


def filter_in_blocks(rows, fir, taps):
    count, length = rows.shape
    tap_limit = fir.shape[1]
    blocks = jnp.transpose(rows.reshape(count, length // 128, 128), (1, 0, 2))
    before = jnp.pad(blocks[:-1], ((1, 0), (0, 0), (0, 0)))
    pieces = jnp.concatenate([before, blocks], axis=2)
    banded = jnp.pad(band_matrix(fir, taps, 128), ((0, 0), (0, 0), (129 - tap_limit, 0)))
    return jnp.einsum(
        "nru,btu->bnrt", pieces, banded, preferred_element_type=jnp.float32
    )


def corr_kernel(off_ref, fw_ref, pp_ref, out_ref, acc_ref, *, widths, groups, scale):
    off = off_ref[0]
    n = acc_ref.shape[2]
    rows_p = n // groups
    src = lax.broadcasted_iota(jnp.int32, (n, n), 0)
    dst = lax.broadcasted_iota(jnp.int32, (n, n), 1)
    perm = ((src % rows_p) * groups + src // rows_p == dst).astype(jnp.bfloat16)
    for band in range(acc_ref.shape[0]):
        acc_ref[band] = jnp.zeros(acc_ref.shape[1:], acc_ref.dtype)
        first = 0
        for width in widths:
            per = width // 128
            fa = jnp.concatenate([fw_ref[band, off + first + i] for i in range(per + 1)], axis=1)
            pa = jnp.concatenate([pp_ref[band, first + i] for i in range(per + 1)], axis=1)
            lhs = jnp.concatenate([fa[:, q : q + width] for q in range(SHIFTS)], axis=0)
            rhs = jnp.concatenate(
                [pa[:, 128 - g * SHIFTS : 128 - g * SHIFTS + width] for g in range(groups)], axis=0
            )
            acc_ref[band] += lax.dot_general(
                lhs, rhs, (((1,), (1,)), ((), ())), preferred_element_type=jnp.float32
            )
            first += per
        rounded = (acc_ref[band] * scale).astype(jnp.bfloat16)
        out_ref[band] = jnp.dot(rounded, perm, preferred_element_type=jnp.float32).astype(
            out_ref.dtype
        )


def correlate(offset, f_blocks, p_blocks, lags, chunks, scale, span):
    bands, nf, rows_f, _ = f_blocks.shape
    np_, rows_p = p_blocks.shape[1], p_blocks.shape[2]
    groups = lags // SHIFTS
    needed = -(-span // 128)
    base, extra = divmod(needed, chunks)
    widths = tuple((base + (i >= chunks - extra)) * 128 for i in range(chunks))
    kernel = functools.partial(corr_kernel, widths=widths, groups=groups, scale=scale)
    m = SHIFTS * rows_f
    n = groups * rows_p
    grid_spec = pltpu.PrefetchScalarGridSpec(
        num_scalar_prefetch=1,
        grid=(bands // PAIR,),
        in_specs=[
            pl.BlockSpec((PAIR, nf, rows_f, 128), lambda b, o: (b, 0, 0, 0)),
            pl.BlockSpec((PAIR, np_, rows_p, 128), lambda b, o: (b, 0, 0, 0)),
        ],
        out_specs=pl.BlockSpec((PAIR, m, n), lambda b, o: (b, 0, 0)),
        scratch_shapes=[pltpu.VMEM((PAIR, m, n), jnp.float32)],
    )
    return pl.pallas_call(
        kernel,
        grid_spec=grid_spec,
        out_shape=jax.ShapeDtypeStruct((bands, m, n), jnp.bfloat16),
        compiler_params=pltpu.CompilerParams(vmem_limit_bytes=48 * 1024 * 1024),
    )(offset, f_blocks, p_blocks)


def summed_over(value, axis):
    count = lax.axis_size(axis)
    bits = max(1, (count - 1).bit_length())
    rounds = [list(range(b, min(b + 2, bits))) for b in range(1, bits, 2)][::-1] + [[0]]
    for group in rounds:
        masks = [
            m for m in range(1, count)
            if all((m >> b) & 1 == 0 for b in range(bits) if b not in group)
        ]
        parts = [lax.ppermute(value, axis, [(i, i ^ m) for i in range(count)]) for m in masks]
        value = sum(parts, value)
    return value


def per_device(signal, fir, taps, sources):
    channels = signal.shape[0]
    shards = lax.axis_size("tm")
    samples_all = signal.shape[1] * shards
    lag_count = 2 * MAXLAG
    share = lag_count // shards
    norm_scale = samples_all ** (-0.5)
    groups = share // SHIFTS
    count_src = sources.shape[1]

    flat_src = sources.reshape(-1)
    local_ids = flat_src - lax.axis_index("sta") * channels
    onehot = (local_ids[:, None] == jnp.arange(channels, dtype=jnp.int32)[None, :]).astype(
        jnp.bfloat16
    )
    picks = jnp.dot(onehot, signal, preferred_element_type=jnp.float32).astype(jnp.bfloat16)
    picks = summed_over(picks, "sta")

    def filtered_of(rows):
        rows = lax.all_gather(rows, "tm", axis=1, tiled=True)
        return filter_in_blocks(rows, fir, taps).astype(jnp.bfloat16)

    f_loc = filtered_of(signal)
    p_src = filtered_of(picks)

    span = samples_all + (groups - 1) * SHIFTS
    chunks = -(-span // CHUNK)
    blocks = chunks * CHUNK // 128 + 1
    data_blocks = samples_all // 128
    f_front = MAXLAG // 128
    f_blocks = jnp.pad(
        f_loc, ((0, 0), (f_front, blocks + lag_count // 128 - data_blocks - f_front), (0, 0), (0, 0))
    )
    p_blocks = jnp.pad(p_src, ((0, 0), (1, blocks - data_blocks - 1), (0, 0), (0, 0)))
    offset = (lax.axis_index("tm") * (share // 128)).astype(jnp.int32).reshape(1)

    out = correlate(offset, f_blocks, p_blocks, share, chunks, norm_scale, span)
    bands = out.shape[0]
    out = out.reshape(bands, SHIFTS, channels, ROUNDS, count_src, groups)
    out = jnp.transpose(out, (3, 0, 4, 2, 5, 1))
    return out.reshape(ROUNDS, bands, count_src, channels, share)


def solution(mesh):
    in_specs = (P("sta", "tm"), P(), P(), P())
    out_specs = P(None, None, None, "sta", "tm")
    return jax.shard_map(
        per_device, mesh=mesh, in_specs=in_specs, out_specs=out_specs, check_vma=False
    )
```

```python
import functools

import jax
import jax.numpy as jnp
from jax import lax
from jax.experimental import pallas as pl
from jax.experimental.pallas import tpu as pltpu
from jax.sharding import PartitionSpec as P

ROUNDS = 2
MAXLAG = 256
SHIFTS = 16
CHUNK = 3200


def skew(values, count_rows):
    leading = values.shape[:-1]
    length = values.shape[-1]
    row_width = length + count_rows
    padded = jnp.concatenate([values, jnp.zeros(leading + (count_rows,), values.dtype)], axis=-1)
    repeated = jnp.tile(padded, (1,) * len(leading) + (count_rows,))
    return repeated[..., : count_rows * (row_width - 1)].reshape(
        leading + (count_rows, row_width - 1)
    )


def band_matrix(fir, taps, count_rows):
    tap_limit = fir.shape[1]
    active = jnp.arange(tap_limit, dtype=jnp.int32)[None, :] < taps[:, None]
    coefficients = jnp.where(active, fir, 0.0).astype(jnp.bfloat16)
    return skew(coefficients[:, ::-1], count_rows)


def filter_in_blocks(rows, fir, taps):
    count, length = rows.shape
    tap_limit = fir.shape[1]
    blocks = jnp.transpose(rows.reshape(count, length // 128, 128), (1, 0, 2))
    before = jnp.pad(blocks[:-1], ((1, 0), (0, 0), (0, 0)))
    pieces = jnp.concatenate([before, blocks], axis=2)
    banded = jnp.pad(band_matrix(fir, taps, 128), ((0, 0), (0, 0), (129 - tap_limit, 0)))
    return jnp.einsum(
        "nru,btu->bnrt", pieces, banded, preferred_element_type=jnp.float32
    )


def corr_kernel(off_ref, fw_ref, pp_ref, out_ref, acc_ref, *, widths, groups, scale):
    acc_ref[...] = jnp.zeros_like(acc_ref)
    off = off_ref[0]
    first = 0
    for width in widths:
        per = width // 128
        fa = jnp.concatenate([fw_ref[0, off + first + i] for i in range(per + 1)], axis=1)
        pa = jnp.concatenate([pp_ref[0, first + i] for i in range(per + 1)], axis=1)
        lhs = jnp.concatenate([fa[:, q : q + width] for q in range(SHIFTS)], axis=0)
        rhs = jnp.concatenate(
            [pa[:, 128 - g * SHIFTS : 128 - g * SHIFTS + width] for g in range(groups)], axis=0
        )
        acc_ref[...] += lax.dot_general(
            lhs, rhs, (((1,), (1,)), ((), ())), preferred_element_type=jnp.float32
        )
        first += per

    rounded = (acc_ref[...] * scale).astype(jnp.bfloat16)
    n = rounded.shape[1]
    rows_p = n // groups
    src = lax.broadcasted_iota(jnp.int32, (n, n), 0)
    dst = lax.broadcasted_iota(jnp.int32, (n, n), 1)
    perm = ((src % rows_p) * groups + src // rows_p == dst).astype(jnp.bfloat16)
    out_ref[0] = jnp.dot(rounded, perm, preferred_element_type=jnp.float32).astype(out_ref.dtype)


def correlate(offset, f_blocks, p_blocks, lags, chunks, scale, span):
    bands, nf, rows_f, _ = f_blocks.shape
    np_, rows_p = p_blocks.shape[1], p_blocks.shape[2]
    groups = lags // SHIFTS
    needed = -(-span // 128)
    base, extra = divmod(needed, chunks)
    widths = tuple((base + (i >= chunks - extra)) * 128 for i in range(chunks))
    kernel = functools.partial(corr_kernel, widths=widths, groups=groups, scale=scale)
    m = SHIFTS * rows_f
    n = groups * rows_p
    grid_spec = pltpu.PrefetchScalarGridSpec(
        num_scalar_prefetch=1,
        grid=(bands,),
        in_specs=[
            pl.BlockSpec((1, nf, rows_f, 128), lambda b, o: (b, 0, 0, 0)),
            pl.BlockSpec((1, np_, rows_p, 128), lambda b, o: (b, 0, 0, 0)),
        ],
        out_specs=pl.BlockSpec((1, m, n), lambda b, o: (b, 0, 0)),
        scratch_shapes=[pltpu.VMEM((m, n), jnp.float32)],
    )
    return pl.pallas_call(
        kernel,
        grid_spec=grid_spec,
        out_shape=jax.ShapeDtypeStruct((bands, m, n), jnp.bfloat16),
        compiler_params=pltpu.CompilerParams(vmem_limit_bytes=48 * 1024 * 1024),
    )(offset, f_blocks, p_blocks)


def summed_over(value, axis):
    count = lax.axis_size(axis)
    bits = max(1, (count - 1).bit_length())
    rounds = [list(range(b, min(b + 2, bits))) for b in range(1, bits, 2)][::-1] + [[0]]
    for group in rounds:
        masks = [
            m for m in range(1, count)
            if all((m >> b) & 1 == 0 for b in range(bits) if b not in group)
        ]
        parts = [lax.ppermute(value, axis, [(i, i ^ m) for i in range(count)]) for m in masks]
        value = sum(parts, value)
    return value


def per_device(signal, fir, taps, sources):
    channels = signal.shape[0]
    shards = lax.axis_size("tm")
    samples_all = signal.shape[1] * shards
    lag_count = 2 * MAXLAG
    share = lag_count // shards
    norm_scale = samples_all ** (-0.5)
    groups = share // SHIFTS
    count_src = sources.shape[1]

    flat_src = sources.reshape(-1)
    local_ids = flat_src - lax.axis_index("sta") * channels
    owned = (local_ids >= 0) & (local_ids < channels)
    rows = jnp.take(signal, jnp.clip(local_ids, 0, channels - 1), axis=0)
    picks = jnp.where(owned[:, None], rows, jnp.zeros_like(rows))
    picks = summed_over(picks, "sta")

    def filtered_of(rows):
        rows = lax.all_gather(rows, "tm", axis=1, tiled=True)
        return filter_in_blocks(rows, fir, taps).astype(jnp.bfloat16)

    f_loc = filtered_of(signal)
    p_src = filtered_of(picks)

    span = samples_all + (groups - 1) * SHIFTS
    chunks = -(-span // CHUNK)
    blocks = chunks * CHUNK // 128 + 1
    data_blocks = samples_all // 128
    f_front = MAXLAG // 128
    f_blocks = jnp.pad(
        f_loc, ((0, 0), (f_front, blocks + lag_count // 128 - data_blocks - f_front), (0, 0), (0, 0))
    )
    p_blocks = jnp.pad(p_src, ((0, 0), (1, blocks - data_blocks - 1), (0, 0), (0, 0)))
    offset = (lax.axis_index("tm") * (share // 128)).astype(jnp.int32).reshape(1)

    out = correlate(offset, f_blocks, p_blocks, share, chunks, norm_scale, span)
    bands = out.shape[0]
    out = out.reshape(bands, SHIFTS, channels, ROUNDS, count_src, groups)
    out = jnp.transpose(out, (3, 0, 4, 2, 5, 1))
    return out.reshape(ROUNDS, bands, count_src, channels, share)


def solution(mesh):
    in_specs = (P("sta", "tm"), P(), P(), P())
    out_specs = P(None, None, None, "sta", "tm")
    return jax.shard_map(
        per_device, mesh=mesh, in_specs=in_specs, out_specs=out_specs, check_vma=False
    )
```

```python
import functools

import jax
import jax.numpy as jnp
from jax import lax
from jax.experimental import pallas as pl
from jax.experimental.pallas import tpu as pltpu
from jax.sharding import PartitionSpec as P

ROUNDS = 2
MAXLAG = 256
SHIFTS = 16
CHUNK = 4224


def skew(values, count_rows):
    leading = values.shape[:-1]
    length = values.shape[-1]
    row_width = length + count_rows
    padded = jnp.concatenate([values, jnp.zeros(leading + (count_rows,), values.dtype)], axis=-1)
    repeated = jnp.tile(padded, (1,) * len(leading) + (count_rows,))
    return repeated[..., : count_rows * (row_width - 1)].reshape(
        leading + (count_rows, row_width - 1)
    )


def band_matrix(fir, taps, count_rows):
    tap_limit = fir.shape[1]
    active = jnp.arange(tap_limit, dtype=jnp.int32)[None, :] < taps[:, None]
    coefficients = jnp.where(active, fir, 0.0).astype(jnp.bfloat16)
    return skew(coefficients[:, ::-1], count_rows)


def filter_in_blocks(rows, fir, taps):
    count, length = rows.shape
    tap_limit = fir.shape[1]
    blocks = jnp.transpose(rows.reshape(count, length // 128, 128), (1, 0, 2))
    before = jnp.pad(blocks[:-1], ((1, 0), (0, 0), (0, 0)))
    pieces = jnp.concatenate([before, blocks], axis=2)
    banded = jnp.pad(band_matrix(fir, taps, 128), ((0, 0), (0, 0), (129 - tap_limit, 0)))
    return jnp.einsum(
        "nru,btu->bnrt", pieces, banded, preferred_element_type=jnp.float32
    )


def corr_kernel(off_ref, fw_ref, pp_ref, out_ref, acc_ref, *, widths, groups, scale):
    acc_ref[...] = jnp.zeros_like(acc_ref)
    off = off_ref[0]
    first = 0
    for width in widths:
        per = width // 128
        fa = jnp.concatenate([fw_ref[0, off + first + i] for i in range(per + 1)], axis=1)
        pa = jnp.concatenate([pp_ref[0, first + i] for i in range(per + 1)], axis=1)
        lhs = jnp.concatenate([fa[:, q : q + width] for q in range(SHIFTS)], axis=0)
        rhs = jnp.concatenate(
            [pa[:, 128 - g * SHIFTS : 128 - g * SHIFTS + width] for g in range(groups)], axis=0
        )
        acc_ref[...] += lax.dot_general(
            lhs, rhs, (((1,), (1,)), ((), ())), preferred_element_type=jnp.float32
        )
        first += per

    rounded = (acc_ref[...] * scale).astype(jnp.bfloat16)
    n = rounded.shape[1]
    rows_p = n // groups
    src = lax.broadcasted_iota(jnp.int32, (n, n), 0)
    dst = lax.broadcasted_iota(jnp.int32, (n, n), 1)
    perm = ((src % rows_p) * groups + src // rows_p == dst).astype(jnp.bfloat16)
    out_ref[0] = jnp.dot(rounded, perm, preferred_element_type=jnp.float32).astype(out_ref.dtype)


def correlate(offset, f_blocks, p_blocks, lags, chunks, scale, span):
    bands, nf, rows_f, _ = f_blocks.shape
    np_, rows_p = p_blocks.shape[1], p_blocks.shape[2]
    groups = lags // SHIFTS
    needed = -(-span // 128)
    base, extra = divmod(needed, chunks)
    widths = tuple((base + (i >= chunks - extra)) * 128 for i in range(chunks))
    kernel = functools.partial(corr_kernel, widths=widths, groups=groups, scale=scale)
    m = SHIFTS * rows_f
    n = groups * rows_p
    grid_spec = pltpu.PrefetchScalarGridSpec(
        num_scalar_prefetch=1,
        grid=(bands,),
        in_specs=[
            pl.BlockSpec((1, nf, rows_f, 128), lambda b, o: (b, 0, 0, 0)),
            pl.BlockSpec((1, np_, rows_p, 128), lambda b, o: (b, 0, 0, 0)),
        ],
        out_specs=pl.BlockSpec((1, m, n), lambda b, o: (b, 0, 0)),
        scratch_shapes=[pltpu.VMEM((m, n), jnp.float32)],
    )
    return pl.pallas_call(
        kernel,
        grid_spec=grid_spec,
        out_shape=jax.ShapeDtypeStruct((bands, m, n), jnp.bfloat16),
        compiler_params=pltpu.CompilerParams(vmem_limit_bytes=48 * 1024 * 1024),
    )(offset, f_blocks, p_blocks)


def summed_over(value, axis):
    count = lax.axis_size(axis)
    bits = max(1, (count - 1).bit_length())
    rounds = [list(range(b, min(b + 2, bits))) for b in range(1, bits, 2)][::-1] + [[0]]
    for group in rounds:
        masks = [
            m for m in range(1, count)
            if all((m >> b) & 1 == 0 for b in range(bits) if b not in group)
        ]
        parts = [lax.ppermute(value, axis, [(i, i ^ m) for i in range(count)]) for m in masks]
        value = sum(parts, value)
    return value


def per_device(signal, fir, taps, sources):
    channels = signal.shape[0]
    shards = lax.axis_size("tm")
    samples_all = signal.shape[1] * shards
    lag_count = 2 * MAXLAG
    share = lag_count // shards
    norm_scale = samples_all ** (-0.5)
    groups = share // SHIFTS
    count_src = sources.shape[1]

    flat_src = sources.reshape(-1)
    local_ids = flat_src - lax.axis_index("sta") * channels
    onehot = (local_ids[:, None] == jnp.arange(channels, dtype=jnp.int32)[None, :]).astype(
        jnp.bfloat16
    )
    picks = jnp.dot(onehot, signal, preferred_element_type=jnp.float32).astype(jnp.bfloat16)
    picks = summed_over(picks, "sta")

    def filtered_of(rows):
        rows = lax.all_gather(rows, "tm", axis=1, tiled=True)
        return filter_in_blocks(rows, fir, taps).astype(jnp.bfloat16)

    f_loc = filtered_of(signal)
    p_src = filtered_of(picks)

    span = samples_all + (groups - 1) * SHIFTS
    chunks = -(-span // CHUNK)
    blocks = chunks * CHUNK // 128 + 1
    data_blocks = samples_all // 128
    f_front = MAXLAG // 128
    f_blocks = jnp.pad(
        f_loc, ((0, 0), (f_front, blocks + lag_count // 128 - data_blocks - f_front), (0, 0), (0, 0))
    )
    p_blocks = jnp.pad(p_src, ((0, 0), (1, blocks - data_blocks - 1), (0, 0), (0, 0)))
    offset = (lax.axis_index("tm") * (share // 128)).astype(jnp.int32).reshape(1)

    out = correlate(offset, f_blocks, p_blocks, share, chunks, norm_scale, span)
    bands = out.shape[0]
    out = out.reshape(bands, SHIFTS, channels, ROUNDS, count_src, groups)
    out = jnp.transpose(out, (3, 0, 4, 2, 5, 1))
    return out.reshape(ROUNDS, bands, count_src, channels, share)


def solution(mesh):
    in_specs = (P("sta", "tm"), P(), P(), P())
    out_specs = P(None, None, None, "sta", "tm")
    return jax.shard_map(
        per_device, mesh=mesh, in_specs=in_specs, out_specs=out_specs, check_vma=False
    )
```
